128 devices in a mesh: px: 8 (over z, core), py: 16 (over y, x).
Axes of the slice: x: 4, y: 4, z: 4, core: 2. Of those that a mesh axis runs over, the one named last changes fastest.
Arguments:
- fractions: float32 [4096, 3, 128], P(('px', 'py')), may hold values from 0 to 1
- charge: float32 [4096, 128], P(('px', 'py')), may hold values from -4 to 4
- cell_index: int32 [4096, 128], P(('px', 'py')), may hold values from 0 to 131071
- destination: int32 [4096, 1], P(('px', 'py')), may hold values from 0 to 15; in each aligned block of 32 rows (0 to 31, 32 to 63, ...) at most 3 rows name the same one
- live_blocks: int32 [128], P(('px', 'py')), may hold values from 16 to 32, as said below
Outputs:
- forces: float32 [4096, 3, 128], P(('px', 'py'))
The draws below stay inside these ranges and needn't reach their ends.
Inputs may be any that keep to these rules, and one draw needn't show every extreme that they name: `destination`: in the rows of one device no value is named by more than 3 blocks, a bound that some block reaches. `live_blocks`: some domain has all 32 slots occupied in every draw.
All inputs are finite; a program needn't handle non-finite values.
Results may differ from the reference program's by a relative error of at most 0.0003.
Values sent between devices are 32-bit elements; how exact they have to be, the bound alone decides.
No kernel may reach another device: no remote copies, remote signals or barrier semaphores. Data moves between devices by JAX's collectives and lax.ppermute only.
A program may use at most 128 MiB of HBM per device.

```python
import math
import jax
import jax.numpy as jnp
import numpy as np

K = 256
BLOCK_ROWS = 128
BLK_DEV = 32
CX = 32
CY = 16
CAP = 3
NBLK = 4096
N_PX = 8
N_PY = 16


def draw_live_blocks(key, part):
    counts = jax.random.randint(key, (N_PX * N_PY,), BLK_DEV // 2, BLK_DEV + 1)
    chosen = jax.random.randint(jax.random.fold_in(key, 7), (), 0, N_PX * N_PY)
    return jnp.where(jnp.arange(N_PX * N_PY) == chosen, BLK_DEV, counts).astype(jnp.int32)


def plant(values, own_key, low, largest):
    longest = values.shape.index(max(values.shape))
    spots = []
    for shift in (0, 1):
        where = [jax.random.randint(jax.random.fold_in(own_key, axis), (), 0, length) for axis, length in enumerate(values.shape)]
        where[longest] = (where[longest] + shift) % values.shape[longest]
        spots.append(tuple(where))
    return values.at[spots[0]].set(low).at[spots[1]].set(largest)


def block_levels(own_key, shape, pieces, smallest, top_value):
    factor_of, own = 1.0, jax.random.fold_in(own_key, 6)
    for position, blocks in pieces:
        draws = jnp.exp(jax.random.uniform(jax.random.fold_in(own, position), (blocks,), jnp.float32, smallest / len(pieces), top_value / len(pieces)))
        factor_of = factor_of * jnp.repeat(draws, shape[position] // blocks).reshape([-1 if axis == position else 1 for axis in range(len(shape))])
    return factor_of


def shared_out(rng, own, number, rows, number_of, top, reach, lean):
    order = jax.random.permutation(rng, number_of)
    heavy_load, common = shares(number_of, rows * top, reach, lean, True), shares(number_of, rows * top, reach, lean, False)
    places = jnp.arange(number_of)

    def named(sizes, turn):
        used = int((sizes > 0).sum())
        fixed = max(1, used // 4)
        passed = fixed + (places - fixed + turn * (used - fixed)) % max(1, number_of - fixed)
        return jnp.zeros((number_of,), jnp.int32).at[order[jnp.where(places < fixed, places, passed)]].set(jnp.asarray(sizes, jnp.int32))

    sizes = jnp.where(number % 4 == 0, named(heavy_load, number // 4), named(common, number - number // 4 - 1))
    mixed = jax.random.permutation(jax.random.fold_in(own, 3), number_of)
    source_of, taker = mixed[0:number_of // 2 * 2:2], mixed[1:number_of // 2 * 2:2]
    room = jnp.minimum(sizes[source_of] - 1, reach - sizes[taker]) // 2
    room = jnp.where((source_of == order[0]) | (taker == order[0]) | (sizes[taker] == 0), 0, jnp.maximum(room, 0))
    passed = jax.random.randint(jax.random.fold_in(own, 4), (number_of // 2,), 0, 1 << 20) % (room + 1)
    sizes = sizes.at[source_of].add(-passed).at[taker].add(passed)
    labels = jnp.searchsorted(jnp.cumsum(sizes), jnp.arange(rows * top), side="right").astype(jnp.int32)
    table = labels.reshape(top, rows).T
    table = table[jax.random.permutation(jax.random.fold_in(own, 1), rows)]
    turn = jax.random.randint(jax.random.fold_in(own, 2), (rows, 1), 0, top)
    return jnp.take_along_axis(table, (jnp.arange(top)[None, :] + turn) % top, axis=1)


def shares(number_of, total, limit, skew, full):
    loads = [(1 << 20) // math.isqrt(rank ** skew) + 1 for rank in range(1, number_of + 1)]
    largest = limit if full else min(limit, max(-(-total // number_of), total * loads[0] // sum(loads)))
    least = 1 if total - largest >= number_of - 1 else 0
    holding, spare = [largest] + [least] * (number_of - 1), total - largest - least * (number_of - 1)
    while spare > 0:
        candidates = [i for i in range(1, number_of) if holding[i] < largest] or [i for i in range(1, number_of) if holding[i] < limit]
        pool, budget = sum([loads[i] for i in candidates]), spare
        for i in candidates:
            extra = min(limit - holding[i], max(1, budget * loads[i] // pool), spare)
            holding[i] = holding[i] + extra
            spare = spare - extra
    return np.array(holding)


def centred(own_key, shape, width, most, split=(), kind=jnp.bfloat16):
    entries = jax.random.normal(own_key, shape, jnp.float32) * width
    if len(split) > 0:
        entries = block_levels(own_key, shape, split, -0.22, 0.18) * entries
    return jnp.clip(entries, min=-most, max=most).astype(kind)


def setup_inputs(seed: int = 0) -> dict:
    seeds = jax.random.split(jax.random.key(seed), 6)
    fractions = jnp.clip(1.0 * jax.random.uniform(seeds[0], (NBLK, 3, BLOCK_ROWS), jnp.float32) ** block_levels(seeds[0], (NBLK, 3, BLOCK_ROWS), ((0, 128),), -0.2, 0.2), 0.0, 1.0)
    charge = centred(seeds[1], (NBLK, BLOCK_ROWS), 1.0, 4.0, ((0, 128),), jnp.float32)
    cell_index = plant(jax.random.randint(seeds[2], (NBLK, BLOCK_ROWS), 0, CX * CY * K), jax.random.fold_in(seeds[2], 1), 0, (CX * CY * K) - 1).astype(jnp.int32)
    destination_keys = jax.random.split(jax.random.fold_in(seeds[3], 1), NBLK // BLK_DEV)
    destination_turns = jax.random.permutation(jax.random.fold_in(seeds[3], 3), NBLK // BLK_DEV)
    destination = jax.vmap(lambda own, number: shared_out(jax.random.fold_in(seeds[3], 2), own, number, BLK_DEV, N_PY, 1, CAP, 2))(destination_keys, destination_turns).reshape((NBLK, 1))
    live_blocks = draw_live_blocks(jax.random.fold_in(seeds[5], 71), 0)
    return {"fractions": fractions, "charge": charge, "cell_index": cell_index, "destination": destination, "live_blocks": live_blocks}


EWALD_GAIN = 4.0
EWALD_BETA = 0.6
SPLINE_SUMS = (1.0 / 120.0, 26.0 / 120.0, 66.0 / 120.0, 26.0 / 120.0, 1.0 / 120.0)


def spline_six(u):
    older_values = [1.0 - u, u]
    slopes = []
    for spline_order in range(3, 7):
        newer_values = []
        for k in range(spline_order):
            from_left = older_values[k - 1] if k >= 1 else jnp.zeros_like(u)
            from_right = older_values[k] if k <= spline_order - 2 else jnp.zeros_like(u)
            newer_values.append(((u + (spline_order - 1 - k)) * from_left + (k + 1 - u) * from_right) * (1.0 / (spline_order - 1)))
        if spline_order == 6:
            slopes = [(older_values[k - 1] if k >= 1 else jnp.zeros_like(u)) - (older_values[k] if k <= 4 else jnp.zeros_like(u)) for k in range(6)]
        older_values = newer_values
    return older_values, slopes


def modulus(wave, extent):
    cos_sum = jnp.zeros(wave.shape, jnp.float32)
    sin_sum = jnp.zeros(wave.shape, jnp.float32)
    for j, value in enumerate(SPLINE_SUMS):
        angle = (2.0 * math.pi / extent) * ((wave * j) % extent).astype(jnp.float32)
        cos_sum = cos_sum + value * jnp.cos(angle)
        sin_sum = sin_sum + value * jnp.sin(angle)
    return 1.0 / (cos_sum * cos_sum + sin_sum * sin_sum)


def influence(wave_x, wave_y, wave_z, extent):
    folded_x = jnp.where(2 * wave_x < extent, wave_x, wave_x - extent).astype(jnp.float32) / extent
    folded_y = jnp.where(2 * wave_y < extent, wave_y, wave_y - extent).astype(jnp.float32) / extent
    folded_z = jnp.where(2 * wave_z < extent, wave_z, wave_z - extent).astype(jnp.float32) / extent
    squared = folded_x * folded_x + folded_y * folded_y + folded_z * folded_z
    safe_squared = jnp.where(squared > 0, squared, 1.0)
    value = EWALD_GAIN * jnp.exp(-(math.pi * math.pi) * squared / (EWALD_BETA * EWALD_BETA)) / safe_squared
    value = value * modulus(wave_x, extent) * modulus(wave_y, extent) * modulus(wave_z, extent)
    return jnp.where(squared > 0, value, 0.0)


def reference(fractions, charge, cell_index, destination, live_blocks):
    block_ids = jnp.arange(NBLK, dtype=jnp.int32)
    device_ids = block_ids // BLK_DEV
    alive = (block_ids % BLK_DEV < live_blocks[device_ids]).astype(jnp.float32)
    row_part = device_ids // N_PY
    amounts = (charge * alive[:, None]).reshape(-1)
    cells_flat = cell_index.reshape(-1)
    grid_x = jnp.repeat(row_part, BLOCK_ROWS) * CX + cells_flat // (CY * K)
    grid_y = jnp.repeat(destination[:, 0], BLOCK_ROWS) * CY + (cells_flat // K) % CY
    grid_z = cells_flat % K
    splines_x, slopes_x = spline_six(fractions[:, 0, :].reshape(-1))
    splines_y, slopes_y = spline_six(fractions[:, 1, :].reshape(-1))
    splines_z, slopes_z = spline_six(fractions[:, 2, :].reshape(-1))
    along_z = jnp.stack(splines_z, axis=1)
    slope_z = jnp.stack(slopes_z, axis=1)
    z_index = (grid_z[:, None] + jnp.arange(6, dtype=jnp.int32)[None, :]) % K
    density = jnp.zeros((K, K, K), jnp.float32)
    for a in range(6):
        for b in range(6):
            x_index = (grid_x + a) % K
            y_index = (grid_y + b) % K
            amount = (amounts * splines_x[a] * splines_y[b])[:, None] * along_z
            density = density.at[x_index[:, None], y_index[:, None], z_index].add(amount)
    spectrum = jnp.fft.fftn(density)
    waves = jnp.arange(K, dtype=jnp.int32)
    kernel = influence(waves[:, None, None], waves[None, :, None], waves[None, None, :], K)
    potential = jnp.real(jnp.fft.ifftn(spectrum * kernel)).astype(jnp.float32)
    force_x = jnp.zeros(amounts.shape, jnp.float32)
    force_y = jnp.zeros(amounts.shape, jnp.float32)
    force_z = jnp.zeros(amounts.shape, jnp.float32)
    for a in range(6):
        for b in range(6):
            x_index = (grid_x + a) % K
            y_index = (grid_y + b) % K
            values = potential[x_index[:, None], y_index[:, None], z_index]
            plain = jnp.sum(values * along_z, axis=1)
            sloped = jnp.sum(values * slope_z, axis=1)
            force_x = force_x + slopes_x[a] * splines_y[b] * plain
            force_y = force_y + splines_x[a] * slopes_y[b] * plain
            force_z = force_z + splines_x[a] * splines_y[b] * sloped
    forces = -amounts[None, :] * jnp.stack([force_x, force_y, force_z])
    return forces.reshape(3, NBLK, BLOCK_ROWS).transpose(1, 0, 2)
```

```python
import math

import jax
import jax.numpy as jnp
from jax import lax
from jax.sharding import PartitionSpec as P

K = 256


EWALD_GAIN = 4.0
EWALD_BETA = 0.6
SPLINE_SUMS = (1.0 / 120.0, 26.0 / 120.0, 66.0 / 120.0, 26.0 / 120.0, 1.0 / 120.0)
HIGHEST = lax.Precision.HIGHEST


def swapped(block, axis, bit):
    count = lax.axis_size(axis)
    route = []
    for low in range(count):
        high = low | 1 << bit
        if high != low and high < count:
            route += [(low, high), (high, low)]
    return lax.ppermute(block, axis, route)


def from_behind(value, axis, steps):
    count = lax.axis_size(axis)
    pairs = [(source, (source + steps) % count) for source in range(count)]
    return lax.ppermute(value, axis, pairs)


def spline_six(u):
    older_values = [1.0 - u, u]
    slopes = []
    for spline_order in range(3, 7):
        newer_values = []
        for k in range(spline_order):
            from_left = older_values[k - 1] if k >= 1 else jnp.zeros_like(u)
            from_right = older_values[k] if k <= spline_order - 2 else jnp.zeros_like(u)
            newer_values.append(
                ((u + (spline_order - 1 - k)) * from_left + (k + 1 - u) * from_right)
                * (1.0 / (spline_order - 1))
            )
        if spline_order == 6:
            slopes = [
                (older_values[k - 1] if k >= 1 else jnp.zeros_like(u))
                - (older_values[k] if k <= 4 else jnp.zeros_like(u))
                for k in range(6)
            ]
        older_values = newer_values
    return (older_values, slopes)


def modulus(wave, extent):
    cos_sum = jnp.zeros(wave.shape, jnp.float32)
    sin_sum = jnp.zeros(wave.shape, jnp.float32)
    for j, value in enumerate(SPLINE_SUMS):
        angle = 2.0 * math.pi / extent * (wave * j % extent).astype(jnp.float32)
        cos_sum = cos_sum + value * jnp.cos(angle)
        sin_sum = sin_sum + value * jnp.sin(angle)
    return 1.0 / (cos_sum * cos_sum + sin_sum * sin_sum)


def influence(wave_x, wave_y, wave_z, extent):
    folded_x = jnp.where(2 * wave_x < extent, wave_x, wave_x - extent).astype(jnp.float32) / extent
    folded_y = jnp.where(2 * wave_y < extent, wave_y, wave_y - extent).astype(jnp.float32) / extent
    folded_z = jnp.where(2 * wave_z < extent, wave_z, wave_z - extent).astype(jnp.float32) / extent
    squared = folded_x * folded_x + folded_y * folded_y + folded_z * folded_z
    safe_squared = jnp.where(squared > 0, squared, 1.0)
    value = (
        EWALD_GAIN
        * jnp.exp(-(math.pi * math.pi) * squared / (EWALD_BETA * EWALD_BETA))
        / safe_squared
    )
    value = value * modulus(wave_x, extent) * modulus(wave_y, extent) * modulus(wave_z, extent)
    return jnp.where(squared > 0, value, 0.0)


def wave_tables(extent):
    steps = jnp.arange(extent, dtype=jnp.int32)
    product = steps[:, None] * steps[None, :] % extent
    angle = 2.0 * math.pi / extent * product.astype(jnp.float32)
    return (jnp.cos(angle), jnp.sin(angle))


def local_forward(start, count, parts):
    outputs = jnp.arange(count, dtype=jnp.int32)[:, None]
    inputs = jnp.arange(count, dtype=jnp.int32)[None, :]
    total = parts * count
    product = inputs * (start + parts * outputs) % total
    angle = -2.0 * math.pi / total * product.astype(jnp.float32)
    return (jnp.cos(angle), jnp.sin(angle))


def reverse_bits(index, count_bits):
    result = jnp.zeros((), jnp.int32)
    for b in range(count_bits):
        result = result + ((index >> b & 1) << count_bits - 1 - b)
    return result


def mix_rows(spectrum, mat_cos, mat_sin):

    def apply_matrix(matrix, values):
        return jnp.einsum("sm,myz->syz", matrix, values, precision=HIGHEST)

    real_part, imag_part = (spectrum[0], spectrum[1])
    return jnp.stack(
        [
            apply_matrix(mat_cos, real_part) - apply_matrix(mat_sin, imag_part),
            apply_matrix(mat_cos, imag_part) + apply_matrix(mat_sin, real_part),
        ]
    )


def mix_columns(spectrum, mat_cos, mat_sin):

    def apply_matrix(matrix, values):
        return jnp.einsum("sm,xmz->xsz", matrix, values, precision=HIGHEST)

    real_part, imag_part = (spectrum[0], spectrum[1])
    return jnp.stack(
        [
            apply_matrix(mat_cos, real_part) - apply_matrix(mat_sin, imag_part),
            apply_matrix(mat_cos, imag_part) + apply_matrix(mat_sin, real_part),
        ]
    )


def swap_rows(spectrum, bit_number):
    return swapped(spectrum, "px", bit_number)


def swap_columns(spectrum, bit_number):
    return swapped(spectrum, "py", bit_number)


def butterfly_section(spectrum, index, bit_number, inverse, exchanger):
    upper = index >> bit_number & 1 == 1
    lower = (index & (1 << bit_number) - 1).astype(jnp.float32)
    angle = -2.0 * math.pi / 2 ** (bit_number + 1) * lower
    turn_cos = jnp.cos(angle)
    turn_sin = jnp.sin(angle)
    real_part, imag_part = (spectrum[0], spectrum[1])
    if inverse:
        turned = jnp.stack(
            [
                turn_cos * real_part + turn_sin * imag_part,
                turn_cos * imag_part - turn_sin * real_part,
            ]
        )
        own_value = jnp.where(upper, turned, spectrum)
        partner = exchanger(own_value, bit_number)
        return jnp.where(upper, partner - own_value, own_value + partner)
    partner = exchanger(spectrum, bit_number)
    diff_real = partner[0] - real_part
    diff_imag = partner[1] - imag_part
    turned = jnp.stack(
        [turn_cos * diff_real - turn_sin * diff_imag, turn_sin * diff_real + turn_cos * diff_imag]
    )
    return jnp.where(upper, turned, spectrum + partner)


def complex_turn(apply_matrix, spectrum, mat_cos, mat_sin, inverse):
    real_part, imag_part = (spectrum[0], spectrum[1])
    sign = 1.0 if inverse else -1.0
    return jnp.stack(
        [
            apply_matrix(mat_cos, real_part) - sign * apply_matrix(mat_sin, imag_part),
            apply_matrix(mat_cos, imag_part) + sign * apply_matrix(mat_sin, real_part),
        ]
    )


def transform_rows(spectrum, mat_cos, mat_sin, inverse):

    def apply_matrix(matrix, values):
        return jnp.einsum("sm,myz->syz", matrix, values, precision=HIGHEST)

    return complex_turn(apply_matrix, spectrum, mat_cos, mat_sin, inverse)


def transform_columns(spectrum, mat_cos, mat_sin, inverse):

    def apply_matrix(matrix, values):
        return jnp.einsum("sm,xmz->xsz", matrix, values, precision=HIGHEST)

    return complex_turn(apply_matrix, spectrum, mat_cos, mat_sin, inverse)


def place_table(base, values, span):
    atoms_count = base.shape[0]
    slots_index = jnp.arange(span, dtype=jnp.int32)[:, None]
    table = jnp.zeros((span, atoms_count), jnp.float32)
    for k in range(6):
        table = table + jnp.where(slots_index == (base + k)[None, :], values[k][None, :], 0.0)
    return table


def place_depth(base, values, extent):
    depth_index = jnp.arange(extent, dtype=jnp.int32)[None, :]
    table = jnp.zeros((base.shape[0], extent), jnp.float32)
    for k in range(6):
        table = table + jnp.where(
            depth_index == ((base + k) % extent)[:, None], values[k][:, None], 0.0
        )
    return table


def per_device(fractions, charge, cell_index, destination, live_blocks):
    rows_dev = lax.axis_size("px")
    cols_dev = lax.axis_size("py")
    span_x = K // rows_dev
    span_y = K // cols_dev
    blocks = charge.shape[0]
    width = charge.shape[1]
    capacity = max(2, 3 * blocks // (2 * cols_dev))
    slots = cols_dev * capacity
    group_blocks = 4
    groups = slots // group_blocks
    atoms_group = group_blocks * width
    alive = (jnp.arange(blocks, dtype=jnp.int32) < live_blocks[0]).astype(jnp.float32)
    target = destination[:, 0]
    matches = (target[:, None] == jnp.arange(cols_dev, dtype=jnp.int32)[None, :]).astype(jnp.int32)
    earlier = jnp.cumsum(matches, axis=0) - matches
    position = jnp.sum(earlier * matches, axis=1)
    slot_of = target * capacity + position
    picked = (slot_of[None, :] == jnp.arange(slots, dtype=jnp.int32)[:, None]).astype(jnp.int32)
    source_block = jnp.sum(picked * jnp.arange(blocks, dtype=jnp.int32)[None, :], axis=1)
    used = jnp.sum(picked, axis=1).astype(jnp.float32)
    payload = jnp.concatenate(
        [
            fractions,
            (charge * alive[:, None])[:, None, :],
            cell_index.astype(jnp.float32)[:, None, :],
        ],
        axis=1,
    )
    outgoing = (jnp.take(payload, source_block, axis=0) * used[:, None, None]).reshape(
        cols_dev, capacity, 5, width
    )
    arrived = lax.all_to_all(outgoing, "py", split_axis=0, concat_axis=0, tiled=True)
    grouped = (
        arrived.reshape(groups, group_blocks, 5, width)
        .transpose(0, 2, 1, 3)
        .reshape(groups, 5, atoms_group)
    )

    def deposit(charge_grid, group):
        cell_value = group[4].astype(jnp.int32)
        base_x = cell_value // (span_y * K)
        base_y = cell_value // K % span_y
        base_z = cell_value % K
        splines_x, slopes_x = spline_six(group[0])
        splines_y, slopes_y = spline_six(group[1])
        splines_z, slopes_z = spline_six(group[2])
        table_x = place_table(base_x, splines_x, span_x + 5)
        slope_x = place_table(base_x, slopes_x, span_x + 5)
        table_y = place_table(base_y, splines_y, span_y + 5)
        slope_y = place_table(base_y, slopes_y, span_y + 5)
        table_z = place_depth(base_z, splines_z, K)
        slope_z = place_depth(base_z, slopes_z, K)
        outer_table = (table_x[:, None, :] * table_y[None, :, :]).reshape(-1, atoms_group)
        charge_grid = charge_grid + jnp.dot(
            outer_table, table_z * group[3][:, None], precision=HIGHEST
        )
        return (charge_grid, (table_x, slope_x, table_y, slope_y, table_z, slope_z, group[3]))

    start_grid = jnp.zeros(((span_x + 5) * (span_y + 5), K), jnp.float32)
    extended, stored = lax.scan(deposit, start_grid, grouped)
    extended = extended.reshape(span_x + 5, span_y + 5, K)
    moved_rows = from_behind(extended[span_x:], "px", 1)
    extended = jnp.concatenate([extended[:5] + moved_rows, extended[5:span_x]], axis=0)
    moved_cols = from_behind(extended[:, span_y:], "py", 1)
    charge_grid = jnp.concatenate([extended[:, :5] + moved_cols, extended[:, 5:span_y]], axis=1)
    depth_cos, depth_sin = wave_tables(K)
    flat_grid = charge_grid.reshape(span_x * span_y, K)
    spectrum = jnp.stack(
        [
            jnp.dot(flat_grid, depth_cos, precision=HIGHEST),
            -jnp.dot(flat_grid, depth_sin, precision=HIGHEST),
        ]
    ).reshape(2, span_x, span_y, K)
    index_x = lax.axis_index("px")
    index_y = lax.axis_index("py")
    spectrum = lax.all_to_all(spectrum, "py", split_axis=3, concat_axis=2, tiled=True)
    spectrum = transform_columns(spectrum, depth_cos, depth_sin, False)
    spectrum = lax.all_to_all(spectrum, "px", split_axis=2, concat_axis=1, tiled=True)
    spectrum = transform_rows(spectrum, depth_cos, depth_sin, False)
    span_ky = K // rows_dev
    span_kz = K // cols_dev
    wave_x = jnp.arange(K, dtype=jnp.int32)
    wave_y = index_x * span_ky + jnp.arange(span_ky, dtype=jnp.int32)
    wave_z = index_y * span_kz + jnp.arange(span_kz, dtype=jnp.int32)
    kernel = influence(wave_x[:, None, None], wave_y[None, :, None], wave_z[None, None, :], K) * (
        1.0 / float(K**3)
    )
    spectrum = spectrum * kernel[None]
    spectrum = transform_rows(spectrum, depth_cos, depth_sin, True)
    spectrum = lax.all_to_all(spectrum, "px", split_axis=1, concat_axis=2, tiled=True)
    spectrum = transform_columns(spectrum, depth_cos, depth_sin, True)
    spectrum = lax.all_to_all(spectrum, "py", split_axis=2, concat_axis=3, tiled=True)
    real_flat = spectrum[0].reshape(span_x * span_y, K)
    imag_flat = spectrum[1].reshape(span_x * span_y, K)
    potential = (
        jnp.dot(real_flat, depth_cos, precision=HIGHEST)
        - jnp.dot(imag_flat, depth_sin, precision=HIGHEST)
    ).reshape(span_x, span_y, K)
    lower_rows = from_behind(potential[:5], "px", -1)
    potential = jnp.concatenate([potential, lower_rows], axis=0)
    lower_cols = from_behind(potential[:, :5], "py", -1)
    potential = jnp.concatenate([potential, lower_cols], axis=1).reshape(-1, K)

    def pull(carry, tables):
        table_x, slope_x, table_y, slope_y, table_z, slope_z, amounts = tables
        stacked = jnp.stack(
            [
                table_x[:, None, :] * table_y[None, :, :],
                slope_x[:, None, :] * table_y[None, :, :],
                table_x[:, None, :] * slope_y[None, :, :],
            ]
        ).reshape(3, -1, atoms_group)
        sampled = jnp.einsum("cga,gz->caz", stacked, potential, precision=HIGHEST)
        force_x = -amounts * jnp.sum(sampled[1] * table_z, axis=1)
        force_y = -amounts * jnp.sum(sampled[2] * table_z, axis=1)
        force_z = -amounts * jnp.sum(sampled[0] * slope_z, axis=1)
        return (carry, jnp.stack([force_x, force_y, force_z]))

    _, pulled = lax.scan(pull, jnp.zeros((), jnp.float32), stored)
    pulled = (
        pulled.reshape(groups, 3, group_blocks, width)
        .transpose(0, 2, 1, 3)
        .reshape(cols_dev, capacity, 3, width)
    )
    returned = lax.all_to_all(pulled, "py", split_axis=0, concat_axis=0, tiled=True).reshape(
        slots, 3, width
    )
    return jnp.take(returned, slot_of, axis=0) * alive[:, None, None]


def solution(mesh):
    placed = (
        P(("px", "py"), None, None),
        P(("px", "py"), None),
        P(("px", "py"), None),
        P(("px", "py"), None),
        P(("px", "py")),
    )
    return jax.shard_map(
        per_device,
        mesh=mesh,
        in_specs=placed,
        out_specs=P(("px", "py"), None, None),
        check_vma=False,
    )
```

```python
import math

import jax
import jax.numpy as jnp
from jax import lax
from jax.sharding import PartitionSpec as P

K = 256


EWALD_GAIN = 4.0
EWALD_BETA = 0.6
SPLINE_SUMS = (1.0 / 120.0, 26.0 / 120.0, 66.0 / 120.0, 26.0 / 120.0, 1.0 / 120.0)
HIGHEST = lax.Precision.HIGHEST
HIGH = lax.Precision.HIGH


def swapped(block, axis, bit):
    count = lax.axis_size(axis)
    route = []
    for low in range(count):
        high = low | 1 << bit
        if high != low and high < count:
            route += [(low, high), (high, low)]
    return lax.ppermute(block, axis, route)


def from_behind(value, axis, steps):
    count = lax.axis_size(axis)
    pairs = [(source, (source + steps) % count) for source in range(count)]
    return lax.ppermute(value, axis, pairs)


def spline_six(u):
    older_values = [1.0 - u, u]
    slopes = []
    for spline_order in range(3, 7):
        newer_values = []
        for k in range(spline_order):
            from_left = older_values[k - 1] if k >= 1 else jnp.zeros_like(u)
            from_right = older_values[k] if k <= spline_order - 2 else jnp.zeros_like(u)
            newer_values.append(
                ((u + (spline_order - 1 - k)) * from_left + (k + 1 - u) * from_right)
                * (1.0 / (spline_order - 1))
            )
        if spline_order == 6:
            slopes = [
                (older_values[k - 1] if k >= 1 else jnp.zeros_like(u))
                - (older_values[k] if k <= 4 else jnp.zeros_like(u))
                for k in range(6)
            ]
        older_values = newer_values
    return (older_values, slopes)


def modulus(wave, extent):
    cos_sum = jnp.zeros(wave.shape, jnp.float32)
    sin_sum = jnp.zeros(wave.shape, jnp.float32)
    for j, value in enumerate(SPLINE_SUMS):
        angle = 2.0 * math.pi / extent * (wave * j % extent).astype(jnp.float32)
        cos_sum = cos_sum + value * jnp.cos(angle)
        sin_sum = sin_sum + value * jnp.sin(angle)
    return 1.0 / (cos_sum * cos_sum + sin_sum * sin_sum)


def influence(wave_x, wave_y, wave_z, extent):
    folded_x = jnp.where(2 * wave_x < extent, wave_x, wave_x - extent).astype(jnp.float32) / extent
    folded_y = jnp.where(2 * wave_y < extent, wave_y, wave_y - extent).astype(jnp.float32) / extent
    folded_z = jnp.where(2 * wave_z < extent, wave_z, wave_z - extent).astype(jnp.float32) / extent
    squared = folded_x * folded_x + folded_y * folded_y + folded_z * folded_z
    safe_squared = jnp.where(squared > 0, squared, 1.0)
    value = (
        EWALD_GAIN
        * jnp.exp(-(math.pi * math.pi) * squared / (EWALD_BETA * EWALD_BETA))
        / safe_squared
    )
    value = value * modulus(wave_x, extent) * modulus(wave_y, extent) * modulus(wave_z, extent)
    return jnp.where(squared > 0, value, 0.0)


def wave_tables(extent):
    steps = jnp.arange(extent, dtype=jnp.int32)
    product = steps[:, None] * steps[None, :] % extent
    angle = 2.0 * math.pi / extent * product.astype(jnp.float32)
    return (jnp.cos(angle), jnp.sin(angle))


def local_forward(start, count, parts):
    outputs = jnp.arange(count, dtype=jnp.int32)[:, None]
    inputs = jnp.arange(count, dtype=jnp.int32)[None, :]
    total = parts * count
    product = inputs * (start + parts * outputs) % total
    angle = -2.0 * math.pi / total * product.astype(jnp.float32)
    return (jnp.cos(angle), jnp.sin(angle))


def reverse_bits(index, count_bits):
    result = jnp.zeros((), jnp.int32)
    for b in range(count_bits):
        result = result + ((index >> b & 1) << count_bits - 1 - b)
    return result


def mix_rows(spectrum, mat_cos, mat_sin):

    def apply_matrix(matrix, values):
        return jnp.einsum("sm,myz->syz", matrix, values, precision=HIGHEST)

    real_part, imag_part = (spectrum[0], spectrum[1])
    return jnp.stack(
        [
            apply_matrix(mat_cos, real_part) - apply_matrix(mat_sin, imag_part),
            apply_matrix(mat_cos, imag_part) + apply_matrix(mat_sin, real_part),
        ]
    )


def mix_columns(spectrum, mat_cos, mat_sin):

    def apply_matrix(matrix, values):
        return jnp.einsum("sm,xmz->xsz", matrix, values, precision=HIGHEST)

    real_part, imag_part = (spectrum[0], spectrum[1])
    return jnp.stack(
        [
            apply_matrix(mat_cos, real_part) - apply_matrix(mat_sin, imag_part),
            apply_matrix(mat_cos, imag_part) + apply_matrix(mat_sin, real_part),
        ]
    )


def swap_rows(spectrum, bit_number):
    return swapped(spectrum, "px", bit_number)


def swap_columns(spectrum, bit_number):
    return swapped(spectrum, "py", bit_number)


def butterfly_section(spectrum, index, bit_number, inverse, exchanger):
    upper = index >> bit_number & 1 == 1
    lower = (index & (1 << bit_number) - 1).astype(jnp.float32)
    angle = -2.0 * math.pi / 2 ** (bit_number + 1) * lower
    turn_cos = jnp.cos(angle)
    turn_sin = jnp.sin(angle)
    real_part, imag_part = (spectrum[0], spectrum[1])
    if inverse:
        turned = jnp.stack(
            [
                turn_cos * real_part + turn_sin * imag_part,
                turn_cos * imag_part - turn_sin * real_part,
            ]
        )
        own_value = jnp.where(upper, turned, spectrum)
        partner = exchanger(own_value, bit_number)
        return jnp.where(upper, partner - own_value, own_value + partner)
    partner = exchanger(spectrum, bit_number)
    diff_real = partner[0] - real_part
    diff_imag = partner[1] - imag_part
    turned = jnp.stack(
        [turn_cos * diff_real - turn_sin * diff_imag, turn_sin * diff_real + turn_cos * diff_imag]
    )
    return jnp.where(upper, turned, spectrum + partner)


def complex_turn(apply_matrix, spectrum, mat_cos, mat_sin, inverse):
    real_part, imag_part = (spectrum[0], spectrum[1])
    sign = 1.0 if inverse else -1.0
    return jnp.stack(
        [
            apply_matrix(mat_cos, real_part) - sign * apply_matrix(mat_sin, imag_part),
            apply_matrix(mat_cos, imag_part) + sign * apply_matrix(mat_sin, real_part),
        ]
    )


def transform_rows(spectrum, mat_cos, mat_sin, inverse):

    def apply_matrix(matrix, values):
        return jnp.einsum("sm,myz->syz", matrix, values, precision=HIGHEST)

    return complex_turn(apply_matrix, spectrum, mat_cos, mat_sin, inverse)


def transform_columns(spectrum, mat_cos, mat_sin, inverse):

    def apply_matrix(matrix, values):
        return jnp.einsum("sm,xmz->xsz", matrix, values, precision=HIGHEST)

    return complex_turn(apply_matrix, spectrum, mat_cos, mat_sin, inverse)


def place_table(base, values, span):
    atoms_count = base.shape[0]
    slots_index = jnp.arange(span, dtype=jnp.int32)[:, None]
    table = jnp.zeros((span, atoms_count), jnp.float32)
    for k in range(6):
        table = table + jnp.where(slots_index == (base + k)[None, :], values[k][None, :], 0.0)
    return table


def place_depth(base, values, extent):
    depth_index = jnp.arange(extent, dtype=jnp.int32)[None, :]
    table = jnp.zeros((base.shape[0], extent), jnp.float32)
    for k in range(6):
        table = table + jnp.where(
            depth_index == ((base + k) % extent)[:, None], values[k][:, None], 0.0
        )
    return table


def per_device(fractions, charge, cell_index, destination, live_blocks):
    rows_dev = lax.axis_size("px")
    cols_dev = lax.axis_size("py")
    span_x = K // rows_dev
    span_y = K // cols_dev
    blocks = charge.shape[0]
    width = charge.shape[1]
    capacity = max(2, 3 * blocks // (2 * cols_dev))
    slots = cols_dev * capacity
    alive = (jnp.arange(blocks, dtype=jnp.int32) < live_blocks[0]).astype(jnp.float32)
    target = destination[:, 0]
    matches = (target[:, None] == jnp.arange(cols_dev, dtype=jnp.int32)[None, :]).astype(jnp.int32)
    earlier = jnp.cumsum(matches, axis=0) - matches
    position = jnp.sum(earlier * matches, axis=1)
    slot_of = target * capacity + position
    picked = (slot_of[None, :] == jnp.arange(slots, dtype=jnp.int32)[:, None]).astype(jnp.int32)
    source_block = jnp.sum(picked * jnp.arange(blocks, dtype=jnp.int32)[None, :], axis=1)
    used = jnp.sum(picked, axis=1).astype(jnp.float32)
    payload = jnp.concatenate(
        [
            fractions,
            (charge * alive[:, None])[:, None, :],
            cell_index.astype(jnp.float32)[:, None, :],
        ],
        axis=1,
    )
    outgoing = (jnp.take(payload, source_block, axis=0) * used[:, None, None]).reshape(
        cols_dev, capacity, 5, width
    )
    arrived = lax.all_to_all(outgoing, "py", split_axis=0, concat_axis=0, tiled=True)
    atoms = slots * width
    placed = arrived.reshape(slots, 5, width).transpose(1, 0, 2).reshape(5, atoms)
    cell_value = placed[4].astype(jnp.int32)
    amounts = placed[3]
    base_x = cell_value // (span_y * K)
    base_y = cell_value // K % span_y
    base_z = cell_value % K
    splines_x, slopes_x = spline_six(placed[0])
    splines_y, slopes_y = spline_six(placed[1])
    splines_z, slopes_z = spline_six(placed[2])
    table_x = place_table(base_x, splines_x, span_x + 5)
    slope_x = place_table(base_x, slopes_x, span_x + 5)
    table_y = place_table(base_y, splines_y, span_y + 5)
    slope_y = place_table(base_y, slopes_y, span_y + 5)
    table_z = place_depth(base_z, splines_z, K)
    slope_z = place_depth(base_z, slopes_z, K)
    outer_table = (table_x[:, None, :] * table_y[None, :, :]).reshape(-1, atoms)
    extended = jnp.dot(outer_table, table_z * amounts[:, None], precision=HIGH)
    extended = extended.reshape(span_x + 5, span_y + 5, K)
    moved_rows = from_behind(extended[span_x:], "px", 1)
    extended = jnp.concatenate([extended[:5] + moved_rows, extended[5:span_x]], axis=0)
    moved_cols = from_behind(extended[:, span_y:], "py", 1)
    charge_grid = jnp.concatenate([extended[:, :5] + moved_cols, extended[:, 5:span_y]], axis=1)
    depth_cos, depth_sin = wave_tables(K)
    flat_grid = charge_grid.reshape(span_x * span_y, K)
    spectrum = jnp.stack(
        [
            jnp.dot(flat_grid, depth_cos, precision=HIGHEST),
            -jnp.dot(flat_grid, depth_sin, precision=HIGHEST),
        ]
    ).reshape(2, span_x, span_y, K)
    index_x = lax.axis_index("px")
    index_y = lax.axis_index("py")
    spectrum = lax.all_to_all(spectrum, "py", split_axis=3, concat_axis=2, tiled=True)
    spectrum = transform_columns(spectrum, depth_cos, depth_sin, False)
    spectrum = lax.all_to_all(spectrum, "px", split_axis=2, concat_axis=1, tiled=True)
    spectrum = transform_rows(spectrum, depth_cos, depth_sin, False)
    span_ky = K // rows_dev
    span_kz = K // cols_dev
    wave_x = jnp.arange(K, dtype=jnp.int32)
    wave_y = index_x * span_ky + jnp.arange(span_ky, dtype=jnp.int32)
    wave_z = index_y * span_kz + jnp.arange(span_kz, dtype=jnp.int32)
    kernel = influence(wave_x[:, None, None], wave_y[None, :, None], wave_z[None, None, :], K) * (
        1.0 / float(K**3)
    )
    spectrum = spectrum * kernel[None]
    spectrum = transform_rows(spectrum, depth_cos, depth_sin, True)
    spectrum = lax.all_to_all(spectrum, "px", split_axis=1, concat_axis=2, tiled=True)
    spectrum = transform_columns(spectrum, depth_cos, depth_sin, True)
    spectrum = lax.all_to_all(spectrum, "py", split_axis=2, concat_axis=3, tiled=True)
    real_flat = spectrum[0].reshape(span_x * span_y, K)
    imag_flat = spectrum[1].reshape(span_x * span_y, K)
    potential = (
        jnp.dot(real_flat, depth_cos, precision=HIGHEST)
        - jnp.dot(imag_flat, depth_sin, precision=HIGHEST)
    ).reshape(span_x, span_y, K)
    lower_rows = from_behind(potential[:5], "px", -1)
    potential = jnp.concatenate([potential, lower_rows], axis=0)
    lower_cols = from_behind(potential[:, :5], "py", -1)
    potential = jnp.concatenate([potential, lower_cols], axis=1).reshape(-1, K)

    both_z = jnp.concatenate([table_z, slope_z], axis=0)
    sampled = lax.dot_general(
        potential, both_z, (((1,), (1,)), ((), ())), precision=HIGH
    ).reshape(span_x + 5, span_y + 5, 2, atoms)
    plain = sampled[:, :, 0]
    sloped = sampled[:, :, 1]
    force_x = jnp.sum(slope_x[:, None, :] * table_y[None, :, :] * plain, axis=(0, 1))
    force_y = jnp.sum(table_x[:, None, :] * slope_y[None, :, :] * plain, axis=(0, 1))
    force_z = jnp.sum(table_x[:, None, :] * table_y[None, :, :] * sloped, axis=(0, 1))
    pulled = (-amounts[None, :] * jnp.stack([force_x, force_y, force_z])).reshape(3, slots, width)
    pulled = pulled.transpose(1, 0, 2).reshape(cols_dev, capacity, 3, width)
    returned = lax.all_to_all(pulled, "py", split_axis=0, concat_axis=0, tiled=True).reshape(
        slots, 3, width
    )
    return jnp.take(returned, slot_of, axis=0) * alive[:, None, None]


def solution(mesh):
    placed = (
        P(("px", "py"), None, None),
        P(("px", "py"), None),
        P(("px", "py"), None),
        P(("px", "py"), None),
        P(("px", "py")),
    )
    return jax.shard_map(
        per_device,
        mesh=mesh,
        in_specs=placed,
        out_specs=P(("px", "py"), None, None),
        check_vma=False,
    )
```

```python
import math

import jax
import jax.numpy as jnp
from jax import lax
from jax.sharding import PartitionSpec as P

K = 256


EWALD_GAIN = 4.0
EWALD_BETA = 0.6
SPLINE_SUMS = (1.0 / 120.0, 26.0 / 120.0, 66.0 / 120.0, 26.0 / 120.0, 1.0 / 120.0)
HIGHEST = lax.Precision.HIGHEST
HIGH = lax.Precision.HIGH


def swapped(block, axis, bit):
    count = lax.axis_size(axis)
    route = []
    for low in range(count):
        high = low | 1 << bit
        if high != low and high < count:
            route += [(low, high), (high, low)]
    return lax.ppermute(block, axis, route)


def from_behind(value, axis, steps):
    count = lax.axis_size(axis)
    pairs = [(source, (source + steps) % count) for source in range(count)]
    return lax.ppermute(value, axis, pairs)


def spline_six(u):
    older_values = [1.0 - u, u]
    slopes = []
    for spline_order in range(3, 7):
        newer_values = []
        for k in range(spline_order):
            from_left = older_values[k - 1] if k >= 1 else jnp.zeros_like(u)
            from_right = older_values[k] if k <= spline_order - 2 else jnp.zeros_like(u)
            newer_values.append(
                ((u + (spline_order - 1 - k)) * from_left + (k + 1 - u) * from_right)
                * (1.0 / (spline_order - 1))
            )
        if spline_order == 6:
            slopes = [
                (older_values[k - 1] if k >= 1 else jnp.zeros_like(u))
                - (older_values[k] if k <= 4 else jnp.zeros_like(u))
                for k in range(6)
            ]
        older_values = newer_values
    return (older_values, slopes)


def modulus(wave, extent):
    cos_sum = jnp.zeros(wave.shape, jnp.float32)
    sin_sum = jnp.zeros(wave.shape, jnp.float32)
    for j, value in enumerate(SPLINE_SUMS):
        angle = 2.0 * math.pi / extent * (wave * j % extent).astype(jnp.float32)
        cos_sum = cos_sum + value * jnp.cos(angle)
        sin_sum = sin_sum + value * jnp.sin(angle)
    return 1.0 / (cos_sum * cos_sum + sin_sum * sin_sum)


def influence(wave_x, wave_y, wave_z, extent):
    folded_x = jnp.where(2 * wave_x < extent, wave_x, wave_x - extent).astype(jnp.float32) / extent
    folded_y = jnp.where(2 * wave_y < extent, wave_y, wave_y - extent).astype(jnp.float32) / extent
    folded_z = jnp.where(2 * wave_z < extent, wave_z, wave_z - extent).astype(jnp.float32) / extent
    squared = folded_x * folded_x + folded_y * folded_y + folded_z * folded_z
    safe_squared = jnp.where(squared > 0, squared, 1.0)
    value = (
        EWALD_GAIN
        * jnp.exp(-(math.pi * math.pi) * squared / (EWALD_BETA * EWALD_BETA))
        / safe_squared
    )
    value = value * modulus(wave_x, extent) * modulus(wave_y, extent) * modulus(wave_z, extent)
    return jnp.where(squared > 0, value, 0.0)


def wave_tables(extent):
    steps = jnp.arange(extent, dtype=jnp.int32)
    product = steps[:, None] * steps[None, :] % extent
    angle = 2.0 * math.pi / extent * product.astype(jnp.float32)
    return (jnp.cos(angle), jnp.sin(angle))


def local_forward(start, count, parts):
    outputs = jnp.arange(count, dtype=jnp.int32)[:, None]
    inputs = jnp.arange(count, dtype=jnp.int32)[None, :]
    total = parts * count
    product = inputs * (start + parts * outputs) % total
    angle = -2.0 * math.pi / total * product.astype(jnp.float32)
    return (jnp.cos(angle), jnp.sin(angle))


def reverse_bits(index, count_bits):
    result = jnp.zeros((), jnp.int32)
    for b in range(count_bits):
        result = result + ((index >> b & 1) << count_bits - 1 - b)
    return result


def mix_rows(spectrum, mat_cos, mat_sin):

    def apply_matrix(matrix, values):
        return jnp.einsum("sm,myz->syz", matrix, values, precision=HIGH)

    real_part, imag_part = (spectrum[0], spectrum[1])
    return jnp.stack(
        [
            apply_matrix(mat_cos, real_part) - apply_matrix(mat_sin, imag_part),
            apply_matrix(mat_cos, imag_part) + apply_matrix(mat_sin, real_part),
        ]
    )


def mix_columns(spectrum, mat_cos, mat_sin):

    def apply_matrix(matrix, values):
        return jnp.einsum("sm,xmz->xsz", matrix, values, precision=HIGH)

    real_part, imag_part = (spectrum[0], spectrum[1])
    return jnp.stack(
        [
            apply_matrix(mat_cos, real_part) - apply_matrix(mat_sin, imag_part),
            apply_matrix(mat_cos, imag_part) + apply_matrix(mat_sin, real_part),
        ]
    )


def swap_rows(spectrum, bit_number):
    return swapped(spectrum, "px", bit_number)


def swap_columns(spectrum, bit_number):
    return swapped(spectrum, "py", bit_number)


def butterfly_section(spectrum, index, bit_number, inverse, exchanger):
    upper = index >> bit_number & 1 == 1
    lower = (index & (1 << bit_number) - 1).astype(jnp.float32)
    angle = -2.0 * math.pi / 2 ** (bit_number + 1) * lower
    turn_cos = jnp.cos(angle)
    turn_sin = jnp.sin(angle)
    real_part, imag_part = (spectrum[0], spectrum[1])
    if inverse:
        turned = jnp.stack(
            [
                turn_cos * real_part + turn_sin * imag_part,
                turn_cos * imag_part - turn_sin * real_part,
            ]
        )
        own_value = jnp.where(upper, turned, spectrum)
        partner = exchanger(own_value, bit_number)
        return jnp.where(upper, partner - own_value, own_value + partner)
    partner = exchanger(spectrum, bit_number)
    diff_real = partner[0] - real_part
    diff_imag = partner[1] - imag_part
    turned = jnp.stack(
        [turn_cos * diff_real - turn_sin * diff_imag, turn_sin * diff_real + turn_cos * diff_imag]
    )
    return jnp.where(upper, turned, spectrum + partner)


def complex_turn(apply_matrix, spectrum, mat_cos, mat_sin, inverse):
    real_part, imag_part = (spectrum[0], spectrum[1])
    sign = 1.0 if inverse else -1.0
    return jnp.stack(
        [
            apply_matrix(mat_cos, real_part) - sign * apply_matrix(mat_sin, imag_part),
            apply_matrix(mat_cos, imag_part) + sign * apply_matrix(mat_sin, real_part),
        ]
    )


def transform_rows(spectrum, mat_cos, mat_sin, inverse):

    def apply_matrix(matrix, values):
        return jnp.einsum("sm,myz->syz", matrix, values, precision=HIGH)

    return complex_turn(apply_matrix, spectrum, mat_cos, mat_sin, inverse)


def transform_columns(spectrum, mat_cos, mat_sin, inverse):

    def apply_matrix(matrix, values):
        return jnp.einsum("sm,xmz->xsz", matrix, values, precision=HIGH)

    return complex_turn(apply_matrix, spectrum, mat_cos, mat_sin, inverse)


def place_table(base, values, span):
    atoms_count = base.shape[0]
    slots_index = jnp.arange(span, dtype=jnp.int32)[:, None]
    table = jnp.zeros((span, atoms_count), jnp.float32)
    for k in range(6):
        table = table + jnp.where(slots_index == (base + k)[None, :], values[k][None, :], 0.0)
    return table


def place_depth(base, values, extent):
    depth_index = jnp.arange(extent, dtype=jnp.int32)[None, :]
    table = jnp.zeros((base.shape[0], extent), jnp.float32)
    for k in range(6):
        table = table + jnp.where(
            depth_index == ((base + k) % extent)[:, None], values[k][:, None], 0.0
        )
    return table


def per_device(fractions, charge, cell_index, destination, live_blocks):
    rows_dev = lax.axis_size("px")
    cols_dev = lax.axis_size("py")
    span_x = K // rows_dev
    span_y = K // cols_dev
    blocks = charge.shape[0]
    width = charge.shape[1]
    capacity = max(2, 3 * blocks // (2 * cols_dev))
    slots = cols_dev * capacity
    alive = (jnp.arange(blocks, dtype=jnp.int32) < live_blocks[0]).astype(jnp.float32)
    target = destination[:, 0]
    matches = (target[:, None] == jnp.arange(cols_dev, dtype=jnp.int32)[None, :]).astype(jnp.int32)
    earlier = jnp.cumsum(matches, axis=0) - matches
    position = jnp.sum(earlier * matches, axis=1)
    slot_of = target * capacity + position
    picked = (slot_of[None, :] == jnp.arange(slots, dtype=jnp.int32)[:, None]).astype(jnp.int32)
    source_block = jnp.sum(picked * jnp.arange(blocks, dtype=jnp.int32)[None, :], axis=1)
    used = jnp.sum(picked, axis=1).astype(jnp.float32)
    payload = jnp.concatenate(
        [
            fractions,
            (charge * alive[:, None])[:, None, :],
            cell_index.astype(jnp.float32)[:, None, :],
        ],
        axis=1,
    )
    outgoing = (jnp.take(payload, source_block, axis=0) * used[:, None, None]).reshape(
        cols_dev, capacity, 5, width
    )
    arrived = lax.all_to_all(outgoing, "py", split_axis=0, concat_axis=0, tiled=True)
    atoms = slots * width
    placed = arrived.reshape(slots, 5, width).transpose(1, 0, 2).reshape(5, atoms)
    cell_value = placed[4].astype(jnp.int32)
    amounts = placed[3]
    base_x = cell_value // (span_y * K)
    base_y = cell_value // K % span_y
    base_z = cell_value % K
    splines_x, slopes_x = spline_six(placed[0])
    splines_y, slopes_y = spline_six(placed[1])
    splines_z, slopes_z = spline_six(placed[2])
    table_x = place_table(base_x, splines_x, span_x + 5)
    slope_x = place_table(base_x, slopes_x, span_x + 5)
    pad_y = -(-(span_y + 5) // 8) * 8
    table_y = place_table(base_y, splines_y, pad_y)
    slope_y = place_table(base_y, slopes_y, pad_y)
    table_z = place_depth(base_z, splines_z, K)
    slope_z = place_depth(base_z, slopes_z, K)
    outer_table = (table_x[:, None, :] * table_y[None, :, :]).reshape(-1, atoms)
    extended = jnp.dot(outer_table, table_z * amounts[:, None], precision=HIGH)
    extended = extended.reshape(span_x + 5, pad_y, K)
    moved_rows = from_behind(extended[span_x:], "px", 1)
    extended = jnp.concatenate([extended[:5] + moved_rows, extended[5:span_x]], axis=0)
    moved_cols = from_behind(extended[:, span_y : span_y + 5], "py", 1)
    charge_grid = jnp.concatenate([extended[:, :5] + moved_cols, extended[:, 5:span_y]], axis=1)
    depth_cos, depth_sin = wave_tables(K)
    flat_grid = charge_grid.reshape(span_x * span_y, K)
    spectrum = jnp.stack(
        [
            jnp.dot(flat_grid, depth_cos, precision=HIGH),
            -jnp.dot(flat_grid, depth_sin, precision=HIGH),
        ]
    ).reshape(2, span_x, span_y, K)
    index_x = lax.axis_index("px")
    index_y = lax.axis_index("py")
    spectrum = lax.all_to_all(spectrum, "py", split_axis=3, concat_axis=2, tiled=True)
    spectrum = transform_columns(spectrum, depth_cos, depth_sin, False)
    spectrum = lax.all_to_all(spectrum, "px", split_axis=2, concat_axis=1, tiled=True)
    spectrum = transform_rows(spectrum, depth_cos, depth_sin, False)
    span_ky = K // rows_dev
    span_kz = K // cols_dev
    wave_x = jnp.arange(K, dtype=jnp.int32)
    wave_y = index_x * span_ky + jnp.arange(span_ky, dtype=jnp.int32)
    wave_z = index_y * span_kz + jnp.arange(span_kz, dtype=jnp.int32)
    kernel = influence(wave_x[:, None, None], wave_y[None, :, None], wave_z[None, None, :], K) * (
        1.0 / float(K**3)
    )
    spectrum = spectrum * kernel[None]
    spectrum = transform_rows(spectrum, depth_cos, depth_sin, True)
    spectrum = lax.all_to_all(spectrum, "px", split_axis=1, concat_axis=2, tiled=True)
    spectrum = transform_columns(spectrum, depth_cos, depth_sin, True)
    spectrum = lax.all_to_all(spectrum, "py", split_axis=2, concat_axis=3, tiled=True)
    real_flat = spectrum[0].reshape(span_x * span_y, K)
    imag_flat = spectrum[1].reshape(span_x * span_y, K)
    potential = (
        jnp.dot(real_flat, depth_cos, precision=HIGH)
        - jnp.dot(imag_flat, depth_sin, precision=HIGH)
    ).reshape(span_x, span_y, K)
    lower_rows = from_behind(potential[:5], "px", -1)
    potential = jnp.concatenate([potential, lower_rows], axis=0)
    lower_cols = from_behind(potential[:, :5], "py", -1)
    gap = jnp.zeros((span_x + 5, pad_y - span_y - 5, K), jnp.float32)
    potential = jnp.concatenate([potential, lower_cols, gap], axis=1).reshape(-1, K)

    both_z = jnp.concatenate([table_z, slope_z], axis=0)
    sampled = lax.dot_general(
        potential, both_z, (((1,), (1,)), ((), ())), precision=HIGH
    ).reshape(span_x + 5, pad_y, 2, atoms)
    plain = sampled[:, :, 0]
    sloped = sampled[:, :, 1]
    force_x = jnp.sum(slope_x[:, None, :] * table_y[None, :, :] * plain, axis=(0, 1))
    force_y = jnp.sum(table_x[:, None, :] * slope_y[None, :, :] * plain, axis=(0, 1))
    force_z = jnp.sum(table_x[:, None, :] * table_y[None, :, :] * sloped, axis=(0, 1))
    pulled = (-amounts[None, :] * jnp.stack([force_x, force_y, force_z])).reshape(3, slots, width)
    pulled = pulled.transpose(1, 0, 2).reshape(cols_dev, capacity, 3, width)
    returned = lax.all_to_all(pulled, "py", split_axis=0, concat_axis=0, tiled=True).reshape(
        slots, 3, width
    )
    return jnp.take(returned, slot_of, axis=0) * alive[:, None, None]


def solution(mesh):
    placed = (
        P(("px", "py"), None, None),
        P(("px", "py"), None),
        P(("px", "py"), None),
        P(("px", "py"), None),
        P(("px", "py")),
    )
    return jax.shard_map(
        per_device,
        mesh=mesh,
        in_specs=placed,
        out_specs=P(("px", "py"), None, None),
        check_vma=False,
    )
```

```python
import math

import jax
import jax.numpy as jnp
from jax import lax
from jax.sharding import PartitionSpec as P

K = 256


EWALD_GAIN = 4.0
EWALD_BETA = 0.6
SPLINE_SUMS = (1.0 / 120.0, 26.0 / 120.0, 66.0 / 120.0, 26.0 / 120.0, 1.0 / 120.0)
HIGHEST = lax.Precision.HIGHEST
HIGH = lax.Precision.HIGH


def swapped(block, axis, bit):
    count = lax.axis_size(axis)
    route = []
    for low in range(count):
        high = low | 1 << bit
        if high != low and high < count:
            route += [(low, high), (high, low)]
    return lax.ppermute(block, axis, route)


def from_behind(value, axis, steps):
    count = lax.axis_size(axis)
    pairs = [(source, (source + steps) % count) for source in range(count)]
    return lax.ppermute(value, axis, pairs)


def spline_six(u):
    older_values = [1.0 - u, u]
    slopes = []
    for spline_order in range(3, 7):
        newer_values = []
        for k in range(spline_order):
            from_left = older_values[k - 1] if k >= 1 else jnp.zeros_like(u)
            from_right = older_values[k] if k <= spline_order - 2 else jnp.zeros_like(u)
            newer_values.append(
                ((u + (spline_order - 1 - k)) * from_left + (k + 1 - u) * from_right)
                * (1.0 / (spline_order - 1))
            )
        if spline_order == 6:
            slopes = [
                (older_values[k - 1] if k >= 1 else jnp.zeros_like(u))
                - (older_values[k] if k <= 4 else jnp.zeros_like(u))
                for k in range(6)
            ]
        older_values = newer_values
    return (older_values, slopes)


def modulus(wave, extent):
    cos_sum = jnp.zeros(wave.shape, jnp.float32)
    sin_sum = jnp.zeros(wave.shape, jnp.float32)
    for j, value in enumerate(SPLINE_SUMS):
        angle = 2.0 * math.pi / extent * (wave * j % extent).astype(jnp.float32)
        cos_sum = cos_sum + value * jnp.cos(angle)
        sin_sum = sin_sum + value * jnp.sin(angle)
    return 1.0 / (cos_sum * cos_sum + sin_sum * sin_sum)


def influence(wave_x, wave_y, wave_z, extent):
    folded_x = jnp.where(2 * wave_x < extent, wave_x, wave_x - extent).astype(jnp.float32) / extent
    folded_y = jnp.where(2 * wave_y < extent, wave_y, wave_y - extent).astype(jnp.float32) / extent
    folded_z = jnp.where(2 * wave_z < extent, wave_z, wave_z - extent).astype(jnp.float32) / extent
    squared = folded_x * folded_x + folded_y * folded_y + folded_z * folded_z
    safe_squared = jnp.where(squared > 0, squared, 1.0)
    value = (
        EWALD_GAIN
        * jnp.exp(-(math.pi * math.pi) * squared / (EWALD_BETA * EWALD_BETA))
        / safe_squared
    )
    value = value * modulus(wave_x, extent) * modulus(wave_y, extent) * modulus(wave_z, extent)
    return jnp.where(squared > 0, value, 0.0)


def wave_tables(extent):
    steps = jnp.arange(extent, dtype=jnp.int32)
    product = steps[:, None] * steps[None, :] % extent
    angle = 2.0 * math.pi / extent * product.astype(jnp.float32)
    return (jnp.cos(angle), jnp.sin(angle))


def local_forward(start, count, parts):
    outputs = jnp.arange(count, dtype=jnp.int32)[:, None]
    inputs = jnp.arange(count, dtype=jnp.int32)[None, :]
    total = parts * count
    product = inputs * (start + parts * outputs) % total
    angle = -2.0 * math.pi / total * product.astype(jnp.float32)
    return (jnp.cos(angle), jnp.sin(angle))


def reverse_bits(index, count_bits):
    result = jnp.zeros((), jnp.int32)
    for b in range(count_bits):
        result = result + ((index >> b & 1) << count_bits - 1 - b)
    return result


def mix_rows(spectrum, mat_cos, mat_sin):

    def apply_matrix(matrix, values):
        return jnp.einsum("sm,myz->syz", matrix, values, precision=HIGH)

    real_part, imag_part = (spectrum[0], spectrum[1])
    return jnp.stack(
        [
            apply_matrix(mat_cos, real_part) - apply_matrix(mat_sin, imag_part),
            apply_matrix(mat_cos, imag_part) + apply_matrix(mat_sin, real_part),
        ]
    )


def mix_columns(spectrum, mat_cos, mat_sin):

    def apply_matrix(matrix, values):
        return jnp.einsum("sm,xmz->xsz", matrix, values, precision=HIGH)

    real_part, imag_part = (spectrum[0], spectrum[1])
    return jnp.stack(
        [
            apply_matrix(mat_cos, real_part) - apply_matrix(mat_sin, imag_part),
            apply_matrix(mat_cos, imag_part) + apply_matrix(mat_sin, real_part),
        ]
    )


def swap_rows(spectrum, bit_number):
    return swapped(spectrum, "px", bit_number)


def swap_columns(spectrum, bit_number):
    return swapped(spectrum, "py", bit_number)


def butterfly_section(spectrum, index, bit_number, inverse, exchanger):
    upper = index >> bit_number & 1 == 1
    lower = (index & (1 << bit_number) - 1).astype(jnp.float32)
    angle = -2.0 * math.pi / 2 ** (bit_number + 1) * lower
    turn_cos = jnp.cos(angle)
    turn_sin = jnp.sin(angle)
    real_part, imag_part = (spectrum[0], spectrum[1])
    if inverse:
        turned = jnp.stack(
            [
                turn_cos * real_part + turn_sin * imag_part,
                turn_cos * imag_part - turn_sin * real_part,
            ]
        )
        own_value = jnp.where(upper, turned, spectrum)
        partner = exchanger(own_value, bit_number)
        return jnp.where(upper, partner - own_value, own_value + partner)
    partner = exchanger(spectrum, bit_number)
    diff_real = partner[0] - real_part
    diff_imag = partner[1] - imag_part
    turned = jnp.stack(
        [turn_cos * diff_real - turn_sin * diff_imag, turn_sin * diff_real + turn_cos * diff_imag]
    )
    return jnp.where(upper, turned, spectrum + partner)


def complex_turn(apply_matrix, spectrum, mat_cos, mat_sin, inverse):
    real_part, imag_part = (spectrum[0], spectrum[1])
    sign = 1.0 if inverse else -1.0
    return jnp.stack(
        [
            apply_matrix(mat_cos, real_part) - sign * apply_matrix(mat_sin, imag_part),
            apply_matrix(mat_cos, imag_part) + sign * apply_matrix(mat_sin, real_part),
        ]
    )


def transform_rows(spectrum, mat_cos, mat_sin, inverse):

    def apply_matrix(matrix, values):
        return jnp.einsum("sm,myz->syz", matrix, values, precision=HIGH)

    return complex_turn(apply_matrix, spectrum, mat_cos, mat_sin, inverse)


def transform_columns(spectrum, mat_cos, mat_sin, inverse):

    def apply_matrix(matrix, values):
        return jnp.einsum("sm,xmz->xsz", matrix, values, precision=HIGH)

    return complex_turn(apply_matrix, spectrum, mat_cos, mat_sin, inverse)


def complex_block(mat_cos, mat_sin, inverse):
    turn_imag = mat_sin if inverse else -mat_sin
    return jnp.stack([jnp.stack([mat_cos, -turn_imag]), jnp.stack([turn_imag, mat_cos])])


def place_table(base, values, span):
    atoms_count = base.shape[0]
    slots_index = jnp.arange(span, dtype=jnp.int32)[:, None]
    table = jnp.zeros((span, atoms_count), jnp.float32)
    for k in range(6):
        table = table + jnp.where(slots_index == (base + k)[None, :], values[k][None, :], 0.0)
    return table


def place_depth(base, values, extent):
    depth_index = jnp.arange(extent, dtype=jnp.int32)[None, :]
    table = jnp.zeros((base.shape[0], extent), jnp.float32)
    for k in range(6):
        table = table + jnp.where(
            depth_index == ((base + k) % extent)[:, None], values[k][:, None], 0.0
        )
    return table


def per_device(fractions, charge, cell_index, destination, live_blocks):
    rows_dev = lax.axis_size("px")
    cols_dev = lax.axis_size("py")
    span_x = K // rows_dev
    span_y = K // cols_dev
    blocks = charge.shape[0]
    width = charge.shape[1]
    capacity = max(2, 3 * blocks // (2 * cols_dev))
    slots = cols_dev * capacity
    alive = (jnp.arange(blocks, dtype=jnp.int32) < live_blocks[0]).astype(jnp.float32)
    target = destination[:, 0]
    matches = (target[:, None] == jnp.arange(cols_dev, dtype=jnp.int32)[None, :]).astype(jnp.int32)
    earlier = jnp.cumsum(matches, axis=0) - matches
    position = jnp.sum(earlier * matches, axis=1)
    slot_of = target * capacity + position
    picked = (slot_of[None, :] == jnp.arange(slots, dtype=jnp.int32)[:, None]).astype(jnp.int32)
    source_block = jnp.sum(picked * jnp.arange(blocks, dtype=jnp.int32)[None, :], axis=1)
    used = jnp.sum(picked, axis=1).astype(jnp.float32)
    payload = jnp.concatenate(
        [
            fractions,
            (charge * alive[:, None])[:, None, :],
            cell_index.astype(jnp.float32)[:, None, :],
        ],
        axis=1,
    )
    outgoing = (jnp.take(payload, source_block, axis=0) * used[:, None, None]).reshape(
        cols_dev, capacity, 5, width
    )
    arrived = lax.all_to_all(outgoing, "py", split_axis=0, concat_axis=0, tiled=True)
    atoms = slots * width
    placed = arrived.reshape(slots, 5, width).transpose(1, 0, 2).reshape(5, atoms)
    cell_value = placed[4].astype(jnp.int32)
    amounts = placed[3]
    base_x = cell_value // (span_y * K)
    base_y = cell_value // K % span_y
    base_z = cell_value % K
    splines_x, slopes_x = spline_six(placed[0])
    splines_y, slopes_y = spline_six(placed[1])
    splines_z, slopes_z = spline_six(placed[2])
    table_x = place_table(base_x, splines_x, span_x + 5)
    slope_x = place_table(base_x, slopes_x, span_x + 5)
    pad_y = -(-(span_y + 5) // 8) * 8
    table_y = place_table(base_y, splines_y, pad_y)
    slope_y = place_table(base_y, slopes_y, pad_y)
    table_z = place_depth(base_z, splines_z, K)
    slope_z = place_depth(base_z, slopes_z, K)
    outer_table = (table_x[:, None, :] * table_y[None, :, :]).reshape(-1, atoms)
    extended = jnp.dot(outer_table, table_z * amounts[:, None], precision=HIGH)
    extended = extended.reshape(span_x + 5, pad_y, K)
    moved_rows = from_behind(extended[span_x:], "px", 1)
    extended = jnp.concatenate([extended[:5] + moved_rows, extended[5:span_x]], axis=0)
    moved_cols = from_behind(extended[:, span_y : span_y + 5], "py", 1)
    charge_grid = jnp.concatenate([extended[:, :5] + moved_cols, extended[:, 5:span_y]], axis=1)
    index_x = lax.axis_index("px")
    index_y = lax.axis_index("py")
    span_ky = K // rows_dev
    span_kz = K // cols_dev
    wave_cos, wave_sin = wave_tables(K)
    ahead_z = jnp.stack([wave_cos, -wave_sin]).reshape(2, cols_dev, span_kz, K)
    flat_grid = charge_grid.reshape(span_x * span_y, K)
    spectrum = jnp.einsum("cjkz,mz->jckm", ahead_z, flat_grid, precision=HIGH)
    spectrum = lax.all_to_all(spectrum, "py", 0, 0, tiled=True)
    spectrum = spectrum.reshape(cols_dev, 2, span_kz, span_x, span_y)
    turn_y = complex_block(wave_cos, wave_sin, False).reshape(2, 2, rows_dev, span_ky, cols_dev, span_y)
    spectrum = jnp.einsum("dcilsy,sckxy->idlkx", turn_y, spectrum, precision=HIGH)
    spectrum = spectrum.reshape(rows_dev, 2, span_ky, span_kz * span_x)
    spectrum = lax.all_to_all(spectrum, "px", 0, 0, tiled=True)
    spectrum = spectrum.reshape(rows_dev, 2, span_ky, span_kz, span_x)
    turn_x = complex_block(wave_cos, wave_sin, False).reshape(2, 2, K, rows_dev, span_x)
    spectrum = jnp.einsum("dcqrx,rclkx->qdlk", turn_x, spectrum, precision=HIGH)
    wave_x = jnp.arange(K, dtype=jnp.int32)
    wave_y = index_x * span_ky + jnp.arange(span_ky, dtype=jnp.int32)
    wave_z = index_y * span_kz + jnp.arange(span_kz, dtype=jnp.int32)
    kernel = influence(wave_x[:, None, None], wave_y[None, :, None], wave_z[None, None, :], K) * (
        1.0 / float(K**3)
    )
    spectrum = spectrum * kernel[:, None]
    back_x = complex_block(wave_cos, wave_sin, True).reshape(2, 2, rows_dev, span_x, K)
    spectrum = jnp.einsum("dcrxq,qclk->rdlkx", back_x, spectrum, precision=HIGH)
    spectrum = spectrum.reshape(rows_dev, 2, span_ky, span_kz * span_x)
    spectrum = lax.all_to_all(spectrum, "px", 0, 0, tiled=True)
    spectrum = spectrum.reshape(rows_dev, 2, span_ky, span_kz, span_x)
    back_y = complex_block(wave_cos, wave_sin, True).reshape(2, 2, cols_dev, span_y, rows_dev, span_ky)
    spectrum = jnp.einsum("dcsyil,iclkx->sdkxy", back_y, spectrum, precision=HIGH)
    spectrum = spectrum.reshape(cols_dev, 2, span_kz, span_x * span_y)
    spectrum = lax.all_to_all(spectrum, "py", 0, 0, tiled=True)
    back_z = jnp.stack([wave_cos, -wave_sin], axis=1).reshape(K, 2, cols_dev, span_kz)
    potential = jnp.einsum("zcjk,jckm->mz", back_z, spectrum, precision=HIGH)
    potential = potential.reshape(span_x, span_y, K)
    lower_rows = from_behind(potential[:5], "px", -1)
    potential = jnp.concatenate([potential, lower_rows], axis=0)
    lower_cols = from_behind(potential[:, :5], "py", -1)
    gap = jnp.zeros((span_x + 5, pad_y - span_y - 5, K), jnp.float32)
    potential = jnp.concatenate([potential, lower_cols, gap], axis=1).reshape(-1, K)

    both_z = jnp.concatenate([table_z, slope_z], axis=0)
    sampled = lax.dot_general(
        potential, both_z, (((1,), (1,)), ((), ())), precision=HIGH
    ).reshape(span_x + 5, pad_y, 2, atoms)
    plain = sampled[:, :, 0]
    sloped = sampled[:, :, 1]
    force_x = jnp.sum(slope_x[:, None, :] * table_y[None, :, :] * plain, axis=(0, 1))
    force_y = jnp.sum(table_x[:, None, :] * slope_y[None, :, :] * plain, axis=(0, 1))
    force_z = jnp.sum(table_x[:, None, :] * table_y[None, :, :] * sloped, axis=(0, 1))
    pulled = (-amounts[None, :] * jnp.stack([force_x, force_y, force_z])).reshape(3, slots, width)
    pulled = pulled.transpose(1, 0, 2).reshape(cols_dev, capacity, 3, width)
    returned = lax.all_to_all(pulled, "py", split_axis=0, concat_axis=0, tiled=True).reshape(
        slots, 3, width
    )
    return jnp.take(returned, slot_of, axis=0) * alive[:, None, None]


def solution(mesh):
    placed = (
        P(("px", "py"), None, None),
        P(("px", "py"), None),
        P(("px", "py"), None),
        P(("px", "py"), None),
        P(("px", "py")),
    )
    return jax.shard_map(
        per_device,
        mesh=mesh,
        in_specs=placed,
        out_specs=P(("px", "py"), None, None),
        check_vma=False,
    )
```

```python
import math

import jax
import jax.numpy as jnp
from jax import lax
from jax.sharding import PartitionSpec as P

K = 256


EWALD_GAIN = 4.0
EWALD_BETA = 0.6
SPLINE_SUMS = (1.0 / 120.0, 26.0 / 120.0, 66.0 / 120.0, 26.0 / 120.0, 1.0 / 120.0)
HIGHEST = lax.Precision.HIGHEST
HIGH = lax.Precision.HIGH


def swapped(block, axis, bit):
    count = lax.axis_size(axis)
    route = []
    for low in range(count):
        high = low | 1 << bit
        if high != low and high < count:
            route += [(low, high), (high, low)]
    return lax.ppermute(block, axis, route)


def from_behind(value, axis, steps):
    count = lax.axis_size(axis)
    pairs = [(source, (source + steps) % count) for source in range(count)]
    return lax.ppermute(value, axis, pairs)


def from_corner(value, steps):
    rows = lax.axis_size("px")
    cols = lax.axis_size("py")
    pairs = [
        (i * cols + j, (i + steps) % rows * cols + (j + steps) % cols)
        for i in range(rows)
        for j in range(cols)
    ]
    return lax.ppermute(value, ("px", "py"), pairs)


def spline_six(u):
    older_values = [1.0 - u, u]
    slopes = []
    for spline_order in range(3, 7):
        newer_values = []
        for k in range(spline_order):
            from_left = older_values[k - 1] if k >= 1 else jnp.zeros_like(u)
            from_right = older_values[k] if k <= spline_order - 2 else jnp.zeros_like(u)
            newer_values.append(
                ((u + (spline_order - 1 - k)) * from_left + (k + 1 - u) * from_right)
                * (1.0 / (spline_order - 1))
            )
        if spline_order == 6:
            slopes = [
                (older_values[k - 1] if k >= 1 else jnp.zeros_like(u))
                - (older_values[k] if k <= 4 else jnp.zeros_like(u))
                for k in range(6)
            ]
        older_values = newer_values
    return (older_values, slopes)


def modulus(wave, extent):
    cos_sum = jnp.zeros(wave.shape, jnp.float32)
    sin_sum = jnp.zeros(wave.shape, jnp.float32)
    for j, value in enumerate(SPLINE_SUMS):
        angle = 2.0 * math.pi / extent * (wave * j % extent).astype(jnp.float32)
        cos_sum = cos_sum + value * jnp.cos(angle)
        sin_sum = sin_sum + value * jnp.sin(angle)
    return 1.0 / (cos_sum * cos_sum + sin_sum * sin_sum)


def influence(wave_x, wave_y, wave_z, extent):
    folded_x = jnp.where(2 * wave_x < extent, wave_x, wave_x - extent).astype(jnp.float32) / extent
    folded_y = jnp.where(2 * wave_y < extent, wave_y, wave_y - extent).astype(jnp.float32) / extent
    folded_z = jnp.where(2 * wave_z < extent, wave_z, wave_z - extent).astype(jnp.float32) / extent
    squared = folded_x * folded_x + folded_y * folded_y + folded_z * folded_z
    safe_squared = jnp.where(squared > 0, squared, 1.0)
    value = (
        EWALD_GAIN
        * jnp.exp(-(math.pi * math.pi) * squared / (EWALD_BETA * EWALD_BETA))
        / safe_squared
    )
    value = value * modulus(wave_x, extent) * modulus(wave_y, extent) * modulus(wave_z, extent)
    return jnp.where(squared > 0, value, 0.0)


def wave_tables(extent):
    steps = jnp.arange(extent, dtype=jnp.int32)
    product = steps[:, None] * steps[None, :] % extent
    angle = 2.0 * math.pi / extent * product.astype(jnp.float32)
    return (jnp.cos(angle), jnp.sin(angle))


def local_forward(start, count, parts):
    outputs = jnp.arange(count, dtype=jnp.int32)[:, None]
    inputs = jnp.arange(count, dtype=jnp.int32)[None, :]
    total = parts * count
    product = inputs * (start + parts * outputs) % total
    angle = -2.0 * math.pi / total * product.astype(jnp.float32)
    return (jnp.cos(angle), jnp.sin(angle))


def reverse_bits(index, count_bits):
    result = jnp.zeros((), jnp.int32)
    for b in range(count_bits):
        result = result + ((index >> b & 1) << count_bits - 1 - b)
    return result


def mix_rows(spectrum, mat_cos, mat_sin):

    def apply_matrix(matrix, values):
        return jnp.einsum("sm,myz->syz", matrix, values, precision=HIGH)

    real_part, imag_part = (spectrum[0], spectrum[1])
    return jnp.stack(
        [
            apply_matrix(mat_cos, real_part) - apply_matrix(mat_sin, imag_part),
            apply_matrix(mat_cos, imag_part) + apply_matrix(mat_sin, real_part),
        ]
    )


def mix_columns(spectrum, mat_cos, mat_sin):

    def apply_matrix(matrix, values):
        return jnp.einsum("sm,xmz->xsz", matrix, values, precision=HIGH)

    real_part, imag_part = (spectrum[0], spectrum[1])
    return jnp.stack(
        [
            apply_matrix(mat_cos, real_part) - apply_matrix(mat_sin, imag_part),
            apply_matrix(mat_cos, imag_part) + apply_matrix(mat_sin, real_part),
        ]
    )


def swap_rows(spectrum, bit_number):
    return swapped(spectrum, "px", bit_number)


def swap_columns(spectrum, bit_number):
    return swapped(spectrum, "py", bit_number)


def butterfly_section(spectrum, index, bit_number, inverse, exchanger):
    upper = index >> bit_number & 1 == 1
    lower = (index & (1 << bit_number) - 1).astype(jnp.float32)
    angle = -2.0 * math.pi / 2 ** (bit_number + 1) * lower
    turn_cos = jnp.cos(angle)
    turn_sin = jnp.sin(angle)
    real_part, imag_part = (spectrum[0], spectrum[1])
    if inverse:
        turned = jnp.stack(
            [
                turn_cos * real_part + turn_sin * imag_part,
                turn_cos * imag_part - turn_sin * real_part,
            ]
        )
        own_value = jnp.where(upper, turned, spectrum)
        partner = exchanger(own_value, bit_number)
        return jnp.where(upper, partner - own_value, own_value + partner)
    partner = exchanger(spectrum, bit_number)
    diff_real = partner[0] - real_part
    diff_imag = partner[1] - imag_part
    turned = jnp.stack(
        [turn_cos * diff_real - turn_sin * diff_imag, turn_sin * diff_real + turn_cos * diff_imag]
    )
    return jnp.where(upper, turned, spectrum + partner)


def complex_turn(apply_matrix, spectrum, mat_cos, mat_sin, inverse):
    real_part, imag_part = (spectrum[0], spectrum[1])
    sign = 1.0 if inverse else -1.0
    return jnp.stack(
        [
            apply_matrix(mat_cos, real_part) - sign * apply_matrix(mat_sin, imag_part),
            apply_matrix(mat_cos, imag_part) + sign * apply_matrix(mat_sin, real_part),
        ]
    )


def transform_rows(spectrum, mat_cos, mat_sin, inverse):

    def apply_matrix(matrix, values):
        return jnp.einsum("sm,myz->syz", matrix, values, precision=HIGH)

    return complex_turn(apply_matrix, spectrum, mat_cos, mat_sin, inverse)


def transform_columns(spectrum, mat_cos, mat_sin, inverse):

    def apply_matrix(matrix, values):
        return jnp.einsum("sm,xmz->xsz", matrix, values, precision=HIGH)

    return complex_turn(apply_matrix, spectrum, mat_cos, mat_sin, inverse)


def complex_block(mat_cos, mat_sin, inverse):
    turn_imag = mat_sin if inverse else -mat_sin
    return jnp.stack([jnp.stack([mat_cos, -turn_imag]), jnp.stack([turn_imag, mat_cos])])


def place_table(base, values, span):
    atoms_count = base.shape[0]
    slots_index = jnp.arange(span, dtype=jnp.int32)[:, None]
    table = jnp.zeros((span, atoms_count), jnp.float32)
    for k in range(6):
        table = table + jnp.where(slots_index == (base + k)[None, :], values[k][None, :], 0.0)
    return table


def place_depth(base, values, extent):
    depth_index = jnp.arange(extent, dtype=jnp.int32)[None, :]
    table = jnp.zeros((base.shape[0], extent), jnp.float32)
    for k in range(6):
        table = table + jnp.where(
            depth_index == ((base + k) % extent)[:, None], values[k][:, None], 0.0
        )
    return table


def per_device(fractions, charge, cell_index, destination, live_blocks):
    rows_dev = lax.axis_size("px")
    cols_dev = lax.axis_size("py")
    span_x = K // rows_dev
    span_y = K // cols_dev
    blocks = charge.shape[0]
    width = charge.shape[1]
    capacity = max(2, 3 * blocks // (2 * cols_dev))
    slots = cols_dev * capacity
    alive = (jnp.arange(blocks, dtype=jnp.int32) < live_blocks[0]).astype(jnp.float32)
    target = destination[:, 0]
    matches = (target[:, None] == jnp.arange(cols_dev, dtype=jnp.int32)[None, :]).astype(jnp.int32)
    earlier = jnp.cumsum(matches, axis=0) - matches
    position = jnp.sum(earlier * matches, axis=1)
    slot_of = target * capacity + position
    picked = (slot_of[None, :] == jnp.arange(slots, dtype=jnp.int32)[:, None]).astype(jnp.int32)
    source_block = jnp.sum(picked * jnp.arange(blocks, dtype=jnp.int32)[None, :], axis=1)
    used = jnp.sum(picked, axis=1).astype(jnp.float32)
    payload = jnp.concatenate(
        [
            fractions,
            (charge * alive[:, None])[:, None, :],
            cell_index.astype(jnp.float32)[:, None, :],
        ],
        axis=1,
    )
    outgoing = (jnp.take(payload, source_block, axis=0) * used[:, None, None]).reshape(
        cols_dev, capacity, 5, width
    )
    arrived = lax.all_to_all(outgoing, "py", split_axis=0, concat_axis=0, tiled=True)
    atoms = slots * width
    placed = arrived.reshape(slots, 5, width).transpose(1, 0, 2).reshape(5, atoms)
    cell_value = placed[4].astype(jnp.int32)
    amounts = placed[3]
    base_x = cell_value // (span_y * K)
    base_y = cell_value // K % span_y
    base_z = cell_value % K
    splines_x, slopes_x = spline_six(placed[0])
    splines_y, slopes_y = spline_six(placed[1])
    splines_z, slopes_z = spline_six(placed[2])
    table_x = place_table(base_x, splines_x, span_x + 5)
    slope_x = place_table(base_x, slopes_x, span_x + 5)
    pad_y = -(-(span_y + 5) // 8) * 8
    table_y = place_table(base_y, splines_y, pad_y)
    slope_y = place_table(base_y, slopes_y, pad_y)
    both_z = place_depth(
        jnp.concatenate([base_z, base_z]),
        [jnp.concatenate([splines_z[k], slopes_z[k]]) for k in range(6)],
        K,
    )
    outer_table = ((table_x * amounts[None, :])[:, None, :] * table_y[None, :, :]).reshape(-1, atoms)
    extended = jnp.dot(outer_table, both_z[:atoms], precision=HIGH)
    extended = extended.reshape(span_x + 5, pad_y, K)
    moved_rows = from_behind(extended[span_x:, :span_y], "px", 1)
    moved_cols = from_behind(extended[:span_x, span_y : span_y + 5], "py", 1)
    moved_corner = from_corner(extended[span_x:, span_y : span_y + 5], 1)
    charge_grid = extended[:span_x, :span_y]
    charge_grid = charge_grid.at[:5].add(moved_rows)
    charge_grid = charge_grid.at[:, :5].add(moved_cols)
    charge_grid = charge_grid.at[:5, :5].add(moved_corner)
    index_x = lax.axis_index("px")
    index_y = lax.axis_index("py")
    span_ky = K // rows_dev
    span_kz = K // cols_dev
    wave_cos, wave_sin = wave_tables(K)
    ahead_z = jnp.stack([wave_cos, -wave_sin]).reshape(2, cols_dev, span_kz, K)
    flat_grid = charge_grid.reshape(span_x * span_y, K)
    spectrum = jnp.einsum("cjkz,mz->jckm", ahead_z, flat_grid, precision=HIGH)
    spectrum = lax.all_to_all(spectrum, "py", 0, 0, tiled=True)
    spectrum = spectrum.reshape(cols_dev, 2, span_kz, span_x, span_y)
    turn_y = complex_block(wave_cos, wave_sin, False).reshape(2, 2, rows_dev, span_ky, cols_dev, span_y)
    spectrum = jnp.einsum("dcilsy,sckxy->idlkx", turn_y, spectrum, precision=HIGH)
    spectrum = spectrum.reshape(rows_dev, 2, span_ky, span_kz * span_x)
    spectrum = lax.all_to_all(spectrum, "px", 0, 0, tiled=True)
    spectrum = spectrum.reshape(rows_dev, 2, span_ky, span_kz, span_x)
    turn_x = complex_block(wave_cos, wave_sin, False).reshape(2, 2, K, rows_dev, span_x)
    spectrum = jnp.einsum("dcqrx,rclkx->qdlk", turn_x, spectrum, precision=HIGH)
    wave_x = jnp.arange(K, dtype=jnp.int32)
    wave_y = index_x * span_ky + jnp.arange(span_ky, dtype=jnp.int32)
    wave_z = index_y * span_kz + jnp.arange(span_kz, dtype=jnp.int32)
    kernel = influence(wave_x[:, None, None], wave_y[None, :, None], wave_z[None, None, :], K) * (
        1.0 / float(K**3)
    )
    spectrum = spectrum * kernel[:, None]
    back_x = complex_block(wave_cos, wave_sin, True).reshape(2, 2, rows_dev, span_x, K)
    spectrum = jnp.einsum("dcrxq,qclk->rdlkx", back_x, spectrum, precision=HIGH)
    spectrum = spectrum.reshape(rows_dev, 2, span_ky, span_kz * span_x)
    spectrum = lax.all_to_all(spectrum, "px", 0, 0, tiled=True)
    spectrum = spectrum.reshape(rows_dev, 2, span_ky, span_kz, span_x)
    back_y = complex_block(wave_cos, wave_sin, True).reshape(2, 2, cols_dev, span_y, rows_dev, span_ky)
    spectrum = jnp.einsum("dcsyil,iclkx->sdkxy", back_y, spectrum, precision=HIGH)
    spectrum = spectrum.reshape(cols_dev, 2, span_kz, span_x * span_y)
    spectrum = lax.all_to_all(spectrum, "py", 0, 0, tiled=True)
    back_z = jnp.stack([wave_cos, -wave_sin], axis=1).reshape(K, 2, cols_dev, span_kz)
    potential = jnp.einsum("zcjk,jckm->mz", back_z, spectrum, precision=HIGH)
    potential = potential.reshape(span_x, span_y, K)
    lower_rows = from_behind(potential[:5], "px", -1)
    lower_cols = from_behind(potential[:, :5], "py", -1)
    lower_corner = from_corner(potential[:5, :5], -1)
    gap = jnp.zeros((span_x + 5, pad_y - span_y - 5, K), jnp.float32)
    potential = jnp.concatenate(
        [
            jnp.concatenate([potential, lower_rows], axis=0),
            jnp.concatenate([lower_cols, lower_corner], axis=0),
            gap,
        ],
        axis=1,
    ).reshape(-1, K)

    sampled = lax.dot_general(
        potential, both_z, (((1,), (1,)), ((), ())), precision=HIGH
    ).reshape(span_x + 5, pad_y, 2, atoms)
    plain = sampled[:, :, 0]
    sloped = sampled[:, :, 1]
    force_x = jnp.sum(slope_x[:, None, :] * table_y[None, :, :] * plain, axis=(0, 1))
    force_y = jnp.sum(table_x[:, None, :] * slope_y[None, :, :] * plain, axis=(0, 1))
    force_z = jnp.sum(table_x[:, None, :] * table_y[None, :, :] * sloped, axis=(0, 1))
    pulled = (-amounts[None, :] * jnp.stack([force_x, force_y, force_z])).reshape(3, slots, width)
    pulled = pulled.transpose(1, 0, 2).reshape(cols_dev, capacity, 3, width)
    returned = lax.all_to_all(pulled, "py", split_axis=0, concat_axis=0, tiled=True).reshape(
        slots, 3, width
    )
    return jnp.take(returned, slot_of, axis=0) * alive[:, None, None]


def solution(mesh):
    placed = (
        P(("px", "py"), None, None),
        P(("px", "py"), None),
        P(("px", "py"), None),
        P(("px", "py"), None),
        P(("px", "py")),
    )
    return jax.shard_map(
        per_device,
        mesh=mesh,
        in_specs=placed,
        out_specs=P(("px", "py"), None, None),
        check_vma=False,
    )
```

```python
import math

import jax
import jax.numpy as jnp
from jax import lax
from jax.sharding import PartitionSpec as P

K = 256


EWALD_GAIN = 4.0
EWALD_BETA = 0.6
SPLINE_SUMS = (1.0 / 120.0, 26.0 / 120.0, 66.0 / 120.0, 26.0 / 120.0, 1.0 / 120.0)
HIGHEST = lax.Precision.HIGHEST
HIGH = lax.Precision.HIGH


def swapped(block, axis, bit):
    count = lax.axis_size(axis)
    route = []
    for low in range(count):
        high = low | 1 << bit
        if high != low and high < count:
            route += [(low, high), (high, low)]
    return lax.ppermute(block, axis, route)


def from_behind(value, axis, steps):
    count = lax.axis_size(axis)
    pairs = [(source, (source + steps) % count) for source in range(count)]
    return lax.ppermute(value, axis, pairs)


def from_corner(value, steps):
    rows = lax.axis_size("px")
    cols = lax.axis_size("py")
    pairs = [
        (i * cols + j, (i + steps) % rows * cols + (j + steps) % cols)
        for i in range(rows)
        for j in range(cols)
    ]
    return lax.ppermute(value, ("px", "py"), pairs)


def spline_six(u):
    older_values = [1.0 - u, u]
    slopes = []
    for spline_order in range(3, 7):
        newer_values = []
        for k in range(spline_order):
            from_left = older_values[k - 1] if k >= 1 else jnp.zeros_like(u)
            from_right = older_values[k] if k <= spline_order - 2 else jnp.zeros_like(u)
            newer_values.append(
                ((u + (spline_order - 1 - k)) * from_left + (k + 1 - u) * from_right)
                * (1.0 / (spline_order - 1))
            )
        if spline_order == 6:
            slopes = [
                (older_values[k - 1] if k >= 1 else jnp.zeros_like(u))
                - (older_values[k] if k <= 4 else jnp.zeros_like(u))
                for k in range(6)
            ]
        older_values = newer_values
    return (older_values, slopes)


def modulus(wave, extent):
    cos_sum = jnp.zeros(wave.shape, jnp.float32)
    sin_sum = jnp.zeros(wave.shape, jnp.float32)
    for j, value in enumerate(SPLINE_SUMS):
        angle = 2.0 * math.pi / extent * (wave * j % extent).astype(jnp.float32)
        cos_sum = cos_sum + value * jnp.cos(angle)
        sin_sum = sin_sum + value * jnp.sin(angle)
    return 1.0 / (cos_sum * cos_sum + sin_sum * sin_sum)


def influence(wave_x, wave_y, wave_z, extent):
    folded_x = jnp.where(2 * wave_x < extent, wave_x, wave_x - extent).astype(jnp.float32) / extent
    folded_y = jnp.where(2 * wave_y < extent, wave_y, wave_y - extent).astype(jnp.float32) / extent
    folded_z = jnp.where(2 * wave_z < extent, wave_z, wave_z - extent).astype(jnp.float32) / extent
    squared = folded_x * folded_x + folded_y * folded_y + folded_z * folded_z
    safe_squared = jnp.where(squared > 0, squared, 1.0)
    value = (
        EWALD_GAIN
        * jnp.exp(-(math.pi * math.pi) * squared / (EWALD_BETA * EWALD_BETA))
        / safe_squared
    )
    value = value * modulus(wave_x, extent) * modulus(wave_y, extent) * modulus(wave_z, extent)
    return jnp.where(squared > 0, value, 0.0)


def wave_tables(extent):
    steps = jnp.arange(extent, dtype=jnp.int32)
    product = steps[:, None] * steps[None, :] % extent
    angle = 2.0 * math.pi / extent * product.astype(jnp.float32)
    return (jnp.cos(angle), jnp.sin(angle))


def local_forward(start, count, parts):
    outputs = jnp.arange(count, dtype=jnp.int32)[:, None]
    inputs = jnp.arange(count, dtype=jnp.int32)[None, :]
    total = parts * count
    product = inputs * (start + parts * outputs) % total
    angle = -2.0 * math.pi / total * product.astype(jnp.float32)
    return (jnp.cos(angle), jnp.sin(angle))


def reverse_bits(index, count_bits):
    result = jnp.zeros((), jnp.int32)
    for b in range(count_bits):
        result = result + ((index >> b & 1) << count_bits - 1 - b)
    return result


def mix_rows(spectrum, mat_cos, mat_sin):

    def apply_matrix(matrix, values):
        return jnp.einsum("sm,myz->syz", matrix, values, precision=HIGH)

    real_part, imag_part = (spectrum[0], spectrum[1])
    return jnp.stack(
        [
            apply_matrix(mat_cos, real_part) - apply_matrix(mat_sin, imag_part),
            apply_matrix(mat_cos, imag_part) + apply_matrix(mat_sin, real_part),
        ]
    )


def mix_columns(spectrum, mat_cos, mat_sin):

    def apply_matrix(matrix, values):
        return jnp.einsum("sm,xmz->xsz", matrix, values, precision=HIGH)

    real_part, imag_part = (spectrum[0], spectrum[1])
    return jnp.stack(
        [
            apply_matrix(mat_cos, real_part) - apply_matrix(mat_sin, imag_part),
            apply_matrix(mat_cos, imag_part) + apply_matrix(mat_sin, real_part),
        ]
    )


def swap_rows(spectrum, bit_number):
    return swapped(spectrum, "px", bit_number)


def swap_columns(spectrum, bit_number):
    return swapped(spectrum, "py", bit_number)


def butterfly_section(spectrum, index, bit_number, inverse, exchanger):
    upper = index >> bit_number & 1 == 1
    lower = (index & (1 << bit_number) - 1).astype(jnp.float32)
    angle = -2.0 * math.pi / 2 ** (bit_number + 1) * lower
    turn_cos = jnp.cos(angle)
    turn_sin = jnp.sin(angle)
    real_part, imag_part = (spectrum[0], spectrum[1])
    if inverse:
        turned = jnp.stack(
            [
                turn_cos * real_part + turn_sin * imag_part,
                turn_cos * imag_part - turn_sin * real_part,
            ]
        )
        own_value = jnp.where(upper, turned, spectrum)
        partner = exchanger(own_value, bit_number)
        return jnp.where(upper, partner - own_value, own_value + partner)
    partner = exchanger(spectrum, bit_number)
    diff_real = partner[0] - real_part
    diff_imag = partner[1] - imag_part
    turned = jnp.stack(
        [turn_cos * diff_real - turn_sin * diff_imag, turn_sin * diff_real + turn_cos * diff_imag]
    )
    return jnp.where(upper, turned, spectrum + partner)


def complex_turn(apply_matrix, spectrum, mat_cos, mat_sin, inverse):
    real_part, imag_part = (spectrum[0], spectrum[1])
    sign = 1.0 if inverse else -1.0
    return jnp.stack(
        [
            apply_matrix(mat_cos, real_part) - sign * apply_matrix(mat_sin, imag_part),
            apply_matrix(mat_cos, imag_part) + sign * apply_matrix(mat_sin, real_part),
        ]
    )


def transform_rows(spectrum, mat_cos, mat_sin, inverse):

    def apply_matrix(matrix, values):
        return jnp.einsum("sm,myz->syz", matrix, values, precision=HIGH)

    return complex_turn(apply_matrix, spectrum, mat_cos, mat_sin, inverse)


def transform_columns(spectrum, mat_cos, mat_sin, inverse):

    def apply_matrix(matrix, values):
        return jnp.einsum("sm,xmz->xsz", matrix, values, precision=HIGH)

    return complex_turn(apply_matrix, spectrum, mat_cos, mat_sin, inverse)


def complex_block(mat_cos, mat_sin, inverse):
    turn_imag = mat_sin if inverse else -mat_sin
    return jnp.stack([jnp.stack([mat_cos, -turn_imag]), jnp.stack([turn_imag, mat_cos])])


def place_table(base, values, span):
    atoms_count = base.shape[0]
    slots_index = jnp.arange(span, dtype=jnp.int32)[:, None]
    table = jnp.zeros((span, atoms_count), jnp.float32)
    for k in range(6):
        table = table + jnp.where(slots_index == (base + k)[None, :], values[k][None, :], 0.0)
    return table


def place_depth(base, values, extent):
    depth_index = jnp.arange(extent, dtype=jnp.int32)[None, :]
    table = jnp.zeros((base.shape[0], extent), jnp.float32)
    for k in range(6):
        table = table + jnp.where(
            depth_index == ((base + k) % extent)[:, None], values[k][:, None], 0.0
        )
    return table


def per_device(fractions, charge, cell_index, destination, live_blocks):
    rows_dev = lax.axis_size("px")
    cols_dev = lax.axis_size("py")
    span_x = K // rows_dev
    span_y = K // cols_dev
    blocks = charge.shape[0]
    width = charge.shape[1]
    capacity = max(2, 3 * blocks // (2 * cols_dev))
    slots = cols_dev * capacity
    alive = (jnp.arange(blocks, dtype=jnp.int32) < live_blocks[0]).astype(jnp.float32)
    target = destination[:, 0]
    matches = (target[:, None] == jnp.arange(cols_dev, dtype=jnp.int32)[None, :]).astype(jnp.int32)
    earlier = jnp.cumsum(matches, axis=0) - matches
    position = jnp.sum(earlier * matches, axis=1)
    slot_of = target * capacity + position
    picked = (slot_of[None, :] == jnp.arange(slots, dtype=jnp.int32)[:, None]).astype(jnp.int32)
    source_block = jnp.sum(picked * jnp.arange(blocks, dtype=jnp.int32)[None, :], axis=1)
    used = jnp.sum(picked, axis=1).astype(jnp.float32)
    payload = jnp.concatenate(
        [
            fractions,
            (charge * alive[:, None])[:, None, :],
            cell_index.astype(jnp.float32)[:, None, :],
        ],
        axis=1,
    )
    outgoing = (jnp.take(payload, source_block, axis=0) * used[:, None, None]).reshape(
        cols_dev, capacity, 5, width
    )
    arrived = lax.all_to_all(outgoing, "py", split_axis=0, concat_axis=0, tiled=True)
    atoms = slots * width
    placed = arrived.reshape(slots, 5, width).transpose(1, 0, 2).reshape(5, atoms)
    cell_value = placed[4].astype(jnp.int32)
    amounts = placed[3]
    base_x = cell_value // (span_y * K)
    base_y = cell_value // K % span_y
    base_z = cell_value % K
    splines_x, slopes_x = spline_six(placed[0])
    splines_y, slopes_y = spline_six(placed[1])
    splines_z, slopes_z = spline_six(placed[2])
    table_x = place_table(base_x, splines_x, span_x + 5)
    slope_x = place_table(base_x, slopes_x, span_x + 5)
    pad_y = -(-(span_y + 5) // 8) * 8
    table_y = place_table(base_y, splines_y, pad_y)
    slope_y = place_table(base_y, slopes_y, pad_y)
    both_z = place_depth(
        jnp.concatenate([base_z, base_z]),
        [jnp.concatenate([splines_z[k], slopes_z[k]]) for k in range(6)],
        K,
    )
    both_z = lax.optimization_barrier(both_z)
    outer_table = ((table_x * amounts[None, :])[:, None, :] * table_y[None, :, :]).reshape(-1, atoms)
    extended = jnp.dot(outer_table, both_z[:atoms], precision=HIGH)
    extended = extended.reshape(span_x + 5, pad_y, K)
    moved_rows = from_behind(extended[span_x:, :span_y], "px", 1)
    moved_cols = from_behind(extended[:span_x, span_y : span_y + 5], "py", 1)
    moved_corner = from_corner(extended[span_x:, span_y : span_y + 5], 1)
    charge_grid = extended[:span_x, :span_y]
    charge_grid = charge_grid.at[:5].add(moved_rows)
    charge_grid = charge_grid.at[:, :5].add(moved_cols)
    charge_grid = charge_grid.at[:5, :5].add(moved_corner)
    index_x = lax.axis_index("px")
    index_y = lax.axis_index("py")
    span_ky = K // rows_dev
    span_kz = K // cols_dev
    wave_cos, wave_sin = wave_tables(K)
    ahead = complex_block(wave_cos, wave_sin, False)
    behind = complex_block(wave_cos, wave_sin, True)
    ahead_z = jnp.stack([wave_cos, -wave_sin]).reshape(2, cols_dev, span_kz, K)
    ahead_z = ahead_z.transpose(1, 0, 2, 3).reshape(2 * K, K)
    flat_grid = charge_grid.reshape(span_x * span_y, K)
    spectrum = lax.dot_general(ahead_z, flat_grid, (((1,), (1,)), ((), ())), precision=HIGH)
    spectrum = lax.all_to_all(spectrum.reshape(cols_dev, -1, span_x * span_y), "py", 0, 0, tiled=True)
    spectrum = spectrum.reshape(cols_dev, 2, span_kz, span_x, span_y).transpose(1, 0, 4, 2, 3)
    turn_y = ahead.reshape(2, 2, rows_dev, span_ky, K).transpose(2, 0, 3, 1, 4).reshape(2 * K, 2 * K)
    spectrum = jnp.dot(turn_y, spectrum.reshape(2 * K, -1), precision=HIGH)
    spectrum = lax.all_to_all(spectrum.reshape(rows_dev, -1, span_kz * span_x), "px", 0, 0, tiled=True)
    spectrum = spectrum.reshape(rows_dev, 2, span_ky, span_kz, span_x).transpose(1, 0, 4, 2, 3)
    turn_x = ahead.transpose(0, 2, 1, 3).reshape(2 * K, 2 * K)
    spectrum = jnp.dot(turn_x, spectrum.reshape(2 * K, -1), precision=HIGH)
    wave_x = jnp.arange(K, dtype=jnp.int32)
    wave_y = index_x * span_ky + jnp.arange(span_ky, dtype=jnp.int32)
    wave_z = index_y * span_kz + jnp.arange(span_kz, dtype=jnp.int32)
    kernel = influence(wave_x[:, None, None], wave_y[None, :, None], wave_z[None, None, :], K) * (
        1.0 / float(K**3)
    )
    spectrum = spectrum.reshape(2, K, span_ky * span_kz) * kernel.reshape(1, K, span_ky * span_kz)
    back_x = behind.reshape(2, 2, rows_dev, span_x, K).transpose(2, 0, 3, 1, 4).reshape(2 * K, 2 * K)
    spectrum = jnp.dot(back_x, spectrum.reshape(2 * K, -1), precision=HIGH)
    spectrum = lax.all_to_all(spectrum.reshape(rows_dev, -1, span_ky * span_kz), "px", 0, 0, tiled=True)
    spectrum = spectrum.reshape(rows_dev, 2, span_x, span_ky, span_kz).transpose(1, 0, 3, 2, 4)
    back_y = behind.reshape(2, 2, cols_dev, span_y, K).transpose(2, 0, 3, 1, 4).reshape(2 * K, 2 * K)
    spectrum = jnp.dot(back_y, spectrum.reshape(2 * K, -1), precision=HIGH)
    spectrum = lax.all_to_all(spectrum.reshape(cols_dev, -1, span_x * span_kz), "py", 0, 0, tiled=True)
    spectrum = spectrum.reshape(cols_dev, 2, span_y, span_x, span_kz).transpose(1, 0, 4, 3, 2)
    back_z = jnp.stack([wave_cos, -wave_sin], axis=1).reshape(K, 2 * K)
    potential = lax.dot_general(
        spectrum.reshape(2 * K, -1), back_z, (((0,), (1,)), ((), ())), precision=HIGH
    )
    potential = potential.reshape(span_x, span_y, K)
    lower_rows = from_behind(potential[:5], "px", -1)
    lower_cols = from_behind(potential[:, :5], "py", -1)
    lower_corner = from_corner(potential[:5, :5], -1)
    gap = jnp.zeros((span_x + 5, pad_y - span_y - 5, K), jnp.float32)
    potential = jnp.concatenate(
        [
            jnp.concatenate([potential, lower_rows], axis=0),
            jnp.concatenate([lower_cols, lower_corner], axis=0),
            gap,
        ],
        axis=1,
    ).reshape(-1, K)

    sampled = lax.dot_general(
        potential, both_z, (((1,), (1,)), ((), ())), precision=HIGH
    ).reshape(span_x + 5, pad_y, 2, atoms)
    plain = sampled[:, :, 0]
    sloped = sampled[:, :, 1]
    force_x = jnp.sum(slope_x[:, None, :] * table_y[None, :, :] * plain, axis=(0, 1))
    force_y = jnp.sum(table_x[:, None, :] * slope_y[None, :, :] * plain, axis=(0, 1))
    force_z = jnp.sum(table_x[:, None, :] * table_y[None, :, :] * sloped, axis=(0, 1))
    pulled = (-amounts[None, :] * jnp.stack([force_x, force_y, force_z])).reshape(3, slots, width)
    pulled = pulled.transpose(1, 0, 2).reshape(cols_dev, capacity, 3, width)
    returned = lax.all_to_all(pulled, "py", split_axis=0, concat_axis=0, tiled=True).reshape(
        slots, 3, width
    )
    return jnp.take(returned, slot_of, axis=0) * alive[:, None, None]


def solution(mesh):
    placed = (
        P(("px", "py"), None, None),
        P(("px", "py"), None),
        P(("px", "py"), None),
        P(("px", "py"), None),
        P(("px", "py")),
    )
    return jax.shard_map(
        per_device,
        mesh=mesh,
        in_specs=placed,
        out_specs=P(("px", "py"), None, None),
        check_vma=False,
    )
```

```python
import math

import jax
import jax.numpy as jnp
from jax import lax
from jax.sharding import PartitionSpec as P

K = 256


EWALD_GAIN = 4.0
EWALD_BETA = 0.6
SPLINE_SUMS = (1.0 / 120.0, 26.0 / 120.0, 66.0 / 120.0, 26.0 / 120.0, 1.0 / 120.0)
HIGHEST = lax.Precision.HIGHEST
HIGH = lax.Precision.HIGH


def swapped(block, axis, bit):
    count = lax.axis_size(axis)
    route = []
    for low in range(count):
        high = low | 1 << bit
        if high != low and high < count:
            route += [(low, high), (high, low)]
    return lax.ppermute(block, axis, route)


def from_behind(value, axis, steps):
    count = lax.axis_size(axis)
    pairs = [(source, (source + steps) % count) for source in range(count)]
    return lax.ppermute(value, axis, pairs)


def from_corner(value, steps):
    rows = lax.axis_size("px")
    cols = lax.axis_size("py")
    pairs = [
        (i * cols + j, (i + steps) % rows * cols + (j + steps) % cols)
        for i in range(rows)
        for j in range(cols)
    ]
    return lax.ppermute(value, ("px", "py"), pairs)


def spline_six(u):
    older_values = [1.0 - u, u]
    slopes = []
    for spline_order in range(3, 7):
        newer_values = []
        for k in range(spline_order):
            from_left = older_values[k - 1] if k >= 1 else jnp.zeros_like(u)
            from_right = older_values[k] if k <= spline_order - 2 else jnp.zeros_like(u)
            newer_values.append(
                ((u + (spline_order - 1 - k)) * from_left + (k + 1 - u) * from_right)
                * (1.0 / (spline_order - 1))
            )
        if spline_order == 6:
            slopes = [
                (older_values[k - 1] if k >= 1 else jnp.zeros_like(u))
                - (older_values[k] if k <= 4 else jnp.zeros_like(u))
                for k in range(6)
            ]
        older_values = newer_values
    return (older_values, slopes)


def modulus(wave, extent):
    cos_sum = jnp.zeros(wave.shape, jnp.float32)
    sin_sum = jnp.zeros(wave.shape, jnp.float32)
    for j, value in enumerate(SPLINE_SUMS):
        angle = 2.0 * math.pi / extent * (wave * j % extent).astype(jnp.float32)
        cos_sum = cos_sum + value * jnp.cos(angle)
        sin_sum = sin_sum + value * jnp.sin(angle)
    return 1.0 / (cos_sum * cos_sum + sin_sum * sin_sum)


def influence(wave_x, wave_y, wave_z, extent):
    folded_x = jnp.where(2 * wave_x < extent, wave_x, wave_x - extent).astype(jnp.float32) / extent
    folded_y = jnp.where(2 * wave_y < extent, wave_y, wave_y - extent).astype(jnp.float32) / extent
    folded_z = jnp.where(2 * wave_z < extent, wave_z, wave_z - extent).astype(jnp.float32) / extent
    squared = folded_x * folded_x + folded_y * folded_y + folded_z * folded_z
    safe_squared = jnp.where(squared > 0, squared, 1.0)
    value = (
        EWALD_GAIN
        * jnp.exp(-(math.pi * math.pi) * squared / (EWALD_BETA * EWALD_BETA))
        / safe_squared
    )
    value = value * modulus(wave_x, extent) * modulus(wave_y, extent) * modulus(wave_z, extent)
    return jnp.where(squared > 0, value, 0.0)


def wave_tables(extent):
    steps = jnp.arange(extent, dtype=jnp.int32)
    product = steps[:, None] * steps[None, :] % extent
    angle = 2.0 * math.pi / extent * product.astype(jnp.float32)
    return (jnp.cos(angle), jnp.sin(angle))


def local_forward(start, count, parts):
    outputs = jnp.arange(count, dtype=jnp.int32)[:, None]
    inputs = jnp.arange(count, dtype=jnp.int32)[None, :]
    total = parts * count
    product = inputs * (start + parts * outputs) % total
    angle = -2.0 * math.pi / total * product.astype(jnp.float32)
    return (jnp.cos(angle), jnp.sin(angle))


def reverse_bits(index, count_bits):
    result = jnp.zeros((), jnp.int32)
    for b in range(count_bits):
        result = result + ((index >> b & 1) << count_bits - 1 - b)
    return result


def mix_rows(spectrum, mat_cos, mat_sin):

    def apply_matrix(matrix, values):
        return jnp.einsum("sm,myz->syz", matrix, values, precision=HIGH)

    real_part, imag_part = (spectrum[0], spectrum[1])
    return jnp.stack(
        [
            apply_matrix(mat_cos, real_part) - apply_matrix(mat_sin, imag_part),
            apply_matrix(mat_cos, imag_part) + apply_matrix(mat_sin, real_part),
        ]
    )


def mix_columns(spectrum, mat_cos, mat_sin):

    def apply_matrix(matrix, values):
        return jnp.einsum("sm,xmz->xsz", matrix, values, precision=HIGH)

    real_part, imag_part = (spectrum[0], spectrum[1])
    return jnp.stack(
        [
            apply_matrix(mat_cos, real_part) - apply_matrix(mat_sin, imag_part),
            apply_matrix(mat_cos, imag_part) + apply_matrix(mat_sin, real_part),
        ]
    )


def swap_rows(spectrum, bit_number):
    return swapped(spectrum, "px", bit_number)


def swap_columns(spectrum, bit_number):
    return swapped(spectrum, "py", bit_number)


def butterfly_section(spectrum, index, bit_number, inverse, exchanger):
    upper = index >> bit_number & 1 == 1
    lower = (index & (1 << bit_number) - 1).astype(jnp.float32)
    angle = -2.0 * math.pi / 2 ** (bit_number + 1) * lower
    turn_cos = jnp.cos(angle)
    turn_sin = jnp.sin(angle)
    real_part, imag_part = (spectrum[0], spectrum[1])
    if inverse:
        turned = jnp.stack(
            [
                turn_cos * real_part + turn_sin * imag_part,
                turn_cos * imag_part - turn_sin * real_part,
            ]
        )
        own_value = jnp.where(upper, turned, spectrum)
        partner = exchanger(own_value, bit_number)
        return jnp.where(upper, partner - own_value, own_value + partner)
    partner = exchanger(spectrum, bit_number)
    diff_real = partner[0] - real_part
    diff_imag = partner[1] - imag_part
    turned = jnp.stack(
        [turn_cos * diff_real - turn_sin * diff_imag, turn_sin * diff_real + turn_cos * diff_imag]
    )
    return jnp.where(upper, turned, spectrum + partner)


def complex_turn(apply_matrix, spectrum, mat_cos, mat_sin, inverse):
    real_part, imag_part = (spectrum[0], spectrum[1])
    sign = 1.0 if inverse else -1.0
    return jnp.stack(
        [
            apply_matrix(mat_cos, real_part) - sign * apply_matrix(mat_sin, imag_part),
            apply_matrix(mat_cos, imag_part) + sign * apply_matrix(mat_sin, real_part),
        ]
    )


def transform_rows(spectrum, mat_cos, mat_sin, inverse):

    def apply_matrix(matrix, values):
        return jnp.einsum("sm,myz->syz", matrix, values, precision=HIGH)

    return complex_turn(apply_matrix, spectrum, mat_cos, mat_sin, inverse)


def transform_columns(spectrum, mat_cos, mat_sin, inverse):

    def apply_matrix(matrix, values):
        return jnp.einsum("sm,xmz->xsz", matrix, values, precision=HIGH)

    return complex_turn(apply_matrix, spectrum, mat_cos, mat_sin, inverse)


def complex_block(mat_cos, mat_sin, inverse):
    turn_imag = mat_sin if inverse else -mat_sin
    return jnp.stack([jnp.stack([mat_cos, -turn_imag]), jnp.stack([turn_imag, mat_cos])])


def place_table(base, values, span):
    atoms_count = base.shape[0]
    slots_index = jnp.arange(span, dtype=jnp.int32)[:, None]
    table = jnp.zeros((span, atoms_count), jnp.float32)
    for k in range(6):
        table = table + jnp.where(slots_index == (base + k)[None, :], values[k][None, :], 0.0)
    return table


def place_depth(base, values, extent):
    depth_index = jnp.arange(extent, dtype=jnp.int32)[None, :]
    table = jnp.zeros((base.shape[0], extent), jnp.float32)
    for k in range(6):
        table = table + jnp.where(
            depth_index == ((base + k) % extent)[:, None], values[k][:, None], 0.0
        )
    return table


def per_device(fractions, charge, cell_index, destination, live_blocks):
    rows_dev = lax.axis_size("px")
    cols_dev = lax.axis_size("py")
    span_x = K // rows_dev
    span_y = K // cols_dev
    blocks = charge.shape[0]
    width = charge.shape[1]
    capacity = max(2, 3 * blocks // (2 * cols_dev))
    slots = cols_dev * capacity
    alive = (jnp.arange(blocks, dtype=jnp.int32) < live_blocks[0]).astype(jnp.float32)
    target = destination[:, 0]
    matches = (target[:, None] == jnp.arange(cols_dev, dtype=jnp.int32)[None, :]).astype(jnp.int32)
    earlier = jnp.cumsum(matches, axis=0) - matches
    position = jnp.sum(earlier * matches, axis=1)
    slot_of = target * capacity + position
    picked = (slot_of[None, :] == jnp.arange(slots, dtype=jnp.int32)[:, None]).astype(jnp.int32)
    source_block = jnp.sum(picked * jnp.arange(blocks, dtype=jnp.int32)[None, :], axis=1)
    used = jnp.sum(picked, axis=1).astype(jnp.float32)
    payload = jnp.concatenate(
        [
            fractions,
            (charge * alive[:, None])[:, None, :],
            cell_index.astype(jnp.float32)[:, None, :],
        ],
        axis=1,
    )
    outgoing = (jnp.take(payload, source_block, axis=0) * used[:, None, None]).reshape(
        cols_dev, capacity, 5, width
    )
    arrived = lax.all_to_all(outgoing, "py", split_axis=0, concat_axis=0, tiled=True)
    atoms = slots * width
    placed = arrived.reshape(slots, 5, width).transpose(1, 0, 2).reshape(5, atoms)
    cell_value = placed[4].astype(jnp.int32)
    amounts = placed[3]
    base_x = cell_value // (span_y * K)
    base_y = cell_value // K % span_y
    base_z = cell_value % K
    splines_x, slopes_x = spline_six(placed[0])
    splines_y, slopes_y = spline_six(placed[1])
    splines_z, slopes_z = spline_six(placed[2])
    table_x = place_table(base_x, splines_x, span_x + 5)
    slope_x = place_table(base_x, slopes_x, span_x + 5)
    pad_y = -(-(span_y + 5) // 8) * 8
    table_y = place_table(base_y, splines_y, pad_y)
    slope_y = place_table(base_y, slopes_y, pad_y)
    both_z = place_depth(
        jnp.concatenate([base_z, base_z]),
        [jnp.concatenate([splines_z[k], slopes_z[k]]) for k in range(6)],
        K,
    )
    both_z = lax.optimization_barrier(both_z)
    outer_table = ((table_x * amounts[None, :])[:, None, :] * table_y[None, :, :]).reshape(-1, atoms)
    extended = jnp.dot(outer_table, both_z[:atoms], precision=HIGH)
    extended = extended.reshape(span_x + 5, pad_y, K)
    moved_rows = from_behind(extended[span_x:, :span_y], "px", 1)
    moved_cols = from_behind(extended[:span_x, span_y : span_y + 5], "py", 1)
    moved_corner = from_corner(extended[span_x:, span_y : span_y + 5], 1)
    charge_grid = extended[:span_x, :span_y]
    charge_grid = charge_grid.at[:5].add(moved_rows)
    charge_grid = charge_grid.at[:, :5].add(moved_cols)
    charge_grid = charge_grid.at[:5, :5].add(moved_corner)
    index_x = lax.axis_index("px")
    index_y = lax.axis_index("py")
    span_ky = K // rows_dev
    span_kz = K // cols_dev
    wave_cos, wave_sin = wave_tables(K)
    ahead_z = jnp.stack([wave_cos, -wave_sin]).reshape(2, cols_dev, span_kz, K)
    flat_grid = charge_grid.reshape(span_x * span_y, K)
    spectrum = jnp.einsum("cjkz,mz->jckm", ahead_z, flat_grid, precision=HIGH)
    spectrum = lax.all_to_all(spectrum, "py", 0, 0, tiled=True)
    spectrum = spectrum.reshape(cols_dev, 2, span_kz, span_x, span_y)
    turn_y = complex_block(wave_cos, wave_sin, False).reshape(2, 2, rows_dev, span_ky, cols_dev, span_y)
    spectrum = jnp.einsum("dcilsy,sckxy->idlkx", turn_y, spectrum, precision=HIGH)
    spectrum = spectrum.reshape(rows_dev, 2, span_ky, span_kz * span_x)
    spectrum = lax.all_to_all(spectrum, "px", 0, 0, tiled=True)
    spectrum = spectrum.reshape(rows_dev, 2, span_ky, span_kz, span_x)
    turn_x = complex_block(wave_cos, wave_sin, False).reshape(2, 2, K, rows_dev, span_x)
    spectrum = jnp.einsum("dcqrx,rclkx->qdlk", turn_x, spectrum, precision=HIGH)
    wave_x = jnp.arange(K, dtype=jnp.int32)
    wave_y = index_x * span_ky + jnp.arange(span_ky, dtype=jnp.int32)
    wave_z = index_y * span_kz + jnp.arange(span_kz, dtype=jnp.int32)
    kernel = influence(wave_x[:, None, None], wave_y[None, :, None], wave_z[None, None, :], K) * (
        1.0 / float(K**3)
    )
    spectrum = spectrum * kernel[:, None]
    back_x = complex_block(wave_cos, wave_sin, True).reshape(2, 2, rows_dev, span_x, K)
    spectrum = jnp.einsum("dcrxq,qclk->rdlkx", back_x, spectrum, precision=HIGH)
    spectrum = spectrum.reshape(rows_dev, 2, span_ky, span_kz * span_x)
    spectrum = lax.all_to_all(spectrum, "px", 0, 0, tiled=True)
    spectrum = spectrum.reshape(rows_dev, 2, span_ky, span_kz, span_x)
    back_y = complex_block(wave_cos, wave_sin, True).reshape(2, 2, cols_dev, span_y, rows_dev, span_ky)
    spectrum = jnp.einsum("dcsyil,iclkx->sdkxy", back_y, spectrum, precision=HIGH)
    spectrum = spectrum.reshape(cols_dev, 2, span_kz, span_x * span_y)
    spectrum = lax.all_to_all(spectrum, "py", 0, 0, tiled=True)
    back_z = jnp.stack([wave_cos, -wave_sin], axis=1).reshape(K, 2, cols_dev, span_kz)
    potential = jnp.einsum("zcjk,jckm->mz", back_z, spectrum, precision=HIGH)
    potential = potential.reshape(span_x, span_y, K)
    lower_rows = from_behind(potential[:5], "px", -1)
    lower_cols = from_behind(potential[:, :5], "py", -1)
    lower_corner = from_corner(potential[:5, :5], -1)
    gap = jnp.zeros((span_x + 5, pad_y - span_y - 5, K), jnp.float32)
    potential = jnp.concatenate(
        [
            jnp.concatenate([potential, lower_rows], axis=0),
            jnp.concatenate([lower_cols, lower_corner], axis=0),
            gap,
        ],
        axis=1,
    ).reshape(-1, K)
    potential = lax.optimization_barrier(potential)

    sampled = lax.dot_general(
        potential, both_z, (((1,), (1,)), ((), ())), precision=HIGH
    ).reshape(span_x + 5, pad_y, 2, atoms)
    plain = sampled[:, :, 0]
    sloped = sampled[:, :, 1]
    force_x = jnp.sum(slope_x[:, None, :] * table_y[None, :, :] * plain, axis=(0, 1))
    force_y = jnp.sum(table_x[:, None, :] * slope_y[None, :, :] * plain, axis=(0, 1))
    force_z = jnp.sum(table_x[:, None, :] * table_y[None, :, :] * sloped, axis=(0, 1))
    pulled = (-amounts[None, :] * jnp.stack([force_x, force_y, force_z])).reshape(3, slots, width)
    pulled = pulled.transpose(1, 0, 2).reshape(cols_dev, capacity, 3, width)
    returned = lax.all_to_all(pulled, "py", split_axis=0, concat_axis=0, tiled=True).reshape(
        slots, 3, width
    )
    return jnp.take(returned, slot_of, axis=0) * alive[:, None, None]


def solution(mesh):
    placed = (
        P(("px", "py"), None, None),
        P(("px", "py"), None),
        P(("px", "py"), None),
        P(("px", "py"), None),
        P(("px", "py")),
    )
    return jax.shard_map(
        per_device,
        mesh=mesh,
        in_specs=placed,
        out_specs=P(("px", "py"), None, None),
        check_vma=False,
    )
```

```python
import math

import jax
import jax.numpy as jnp
from jax import lax
from jax.sharding import PartitionSpec as P

K = 256


EWALD_GAIN = 4.0
EWALD_BETA = 0.6
SPLINE_SUMS = (1.0 / 120.0, 26.0 / 120.0, 66.0 / 120.0, 26.0 / 120.0, 1.0 / 120.0)
HIGHEST = lax.Precision.HIGHEST
HIGH = lax.Precision.HIGH


def swapped(block, axis, bit):
    count = lax.axis_size(axis)
    route = []
    for low in range(count):
        high = low | 1 << bit
        if high != low and high < count:
            route += [(low, high), (high, low)]
    return lax.ppermute(block, axis, route)


def from_behind(value, axis, steps):
    count = lax.axis_size(axis)
    pairs = [(source, (source + steps) % count) for source in range(count)]
    return lax.ppermute(value, axis, pairs)


def from_corner(value, steps):
    rows = lax.axis_size("px")
    cols = lax.axis_size("py")
    pairs = [
        (i * cols + j, (i + steps) % rows * cols + (j + steps) % cols)
        for i in range(rows)
        for j in range(cols)
    ]
    return lax.ppermute(value, ("px", "py"), pairs)


def spline_six(u):
    older_values = [1.0 - u, u]
    slopes = []
    for spline_order in range(3, 7):
        newer_values = []
        for k in range(spline_order):
            from_left = older_values[k - 1] if k >= 1 else jnp.zeros_like(u)
            from_right = older_values[k] if k <= spline_order - 2 else jnp.zeros_like(u)
            newer_values.append(
                ((u + (spline_order - 1 - k)) * from_left + (k + 1 - u) * from_right)
                * (1.0 / (spline_order - 1))
            )
        if spline_order == 6:
            slopes = [
                (older_values[k - 1] if k >= 1 else jnp.zeros_like(u))
                - (older_values[k] if k <= 4 else jnp.zeros_like(u))
                for k in range(6)
            ]
        older_values = newer_values
    return (older_values, slopes)


def modulus(wave, extent):
    cos_sum = jnp.zeros(wave.shape, jnp.float32)
    sin_sum = jnp.zeros(wave.shape, jnp.float32)
    for j, value in enumerate(SPLINE_SUMS):
        angle = 2.0 * math.pi / extent * (wave * j % extent).astype(jnp.float32)
        cos_sum = cos_sum + value * jnp.cos(angle)
        sin_sum = sin_sum + value * jnp.sin(angle)
    return 1.0 / (cos_sum * cos_sum + sin_sum * sin_sum)


def influence(wave_x, wave_y, wave_z, extent):
    folded_x = jnp.where(2 * wave_x < extent, wave_x, wave_x - extent).astype(jnp.float32) / extent
    folded_y = jnp.where(2 * wave_y < extent, wave_y, wave_y - extent).astype(jnp.float32) / extent
    folded_z = jnp.where(2 * wave_z < extent, wave_z, wave_z - extent).astype(jnp.float32) / extent
    squared = folded_x * folded_x + folded_y * folded_y + folded_z * folded_z
    safe_squared = jnp.where(squared > 0, squared, 1.0)
    value = (
        EWALD_GAIN
        * jnp.exp(-(math.pi * math.pi) * squared / (EWALD_BETA * EWALD_BETA))
        / safe_squared
    )
    value = value * modulus(wave_x, extent) * modulus(wave_y, extent) * modulus(wave_z, extent)
    return jnp.where(squared > 0, value, 0.0)


def wave_tables(extent):
    steps = jnp.arange(extent, dtype=jnp.int32)
    product = steps[:, None] * steps[None, :] % extent
    angle = 2.0 * math.pi / extent * product.astype(jnp.float32)
    return (jnp.cos(angle), jnp.sin(angle))


def local_forward(start, count, parts):
    outputs = jnp.arange(count, dtype=jnp.int32)[:, None]
    inputs = jnp.arange(count, dtype=jnp.int32)[None, :]
    total = parts * count
    product = inputs * (start + parts * outputs) % total
    angle = -2.0 * math.pi / total * product.astype(jnp.float32)
    return (jnp.cos(angle), jnp.sin(angle))


def reverse_bits(index, count_bits):
    result = jnp.zeros((), jnp.int32)
    for b in range(count_bits):
        result = result + ((index >> b & 1) << count_bits - 1 - b)
    return result


def mix_rows(spectrum, mat_cos, mat_sin):

    def apply_matrix(matrix, values):
        return jnp.einsum("sm,myz->syz", matrix, values, precision=HIGH)

    real_part, imag_part = (spectrum[0], spectrum[1])
    return jnp.stack(
        [
            apply_matrix(mat_cos, real_part) - apply_matrix(mat_sin, imag_part),
            apply_matrix(mat_cos, imag_part) + apply_matrix(mat_sin, real_part),
        ]
    )


def mix_columns(spectrum, mat_cos, mat_sin):

    def apply_matrix(matrix, values):
        return jnp.einsum("sm,xmz->xsz", matrix, values, precision=HIGH)

    real_part, imag_part = (spectrum[0], spectrum[1])
    return jnp.stack(
        [
            apply_matrix(mat_cos, real_part) - apply_matrix(mat_sin, imag_part),
            apply_matrix(mat_cos, imag_part) + apply_matrix(mat_sin, real_part),
        ]
    )


def swap_rows(spectrum, bit_number):
    return swapped(spectrum, "px", bit_number)


def swap_columns(spectrum, bit_number):
    return swapped(spectrum, "py", bit_number)


def butterfly_section(spectrum, index, bit_number, inverse, exchanger):
    upper = index >> bit_number & 1 == 1
    lower = (index & (1 << bit_number) - 1).astype(jnp.float32)
    angle = -2.0 * math.pi / 2 ** (bit_number + 1) * lower
    turn_cos = jnp.cos(angle)
    turn_sin = jnp.sin(angle)
    real_part, imag_part = (spectrum[0], spectrum[1])
    if inverse:
        turned = jnp.stack(
            [
                turn_cos * real_part + turn_sin * imag_part,
                turn_cos * imag_part - turn_sin * real_part,
            ]
        )
        own_value = jnp.where(upper, turned, spectrum)
        partner = exchanger(own_value, bit_number)
        return jnp.where(upper, partner - own_value, own_value + partner)
    partner = exchanger(spectrum, bit_number)
    diff_real = partner[0] - real_part
    diff_imag = partner[1] - imag_part
    turned = jnp.stack(
        [turn_cos * diff_real - turn_sin * diff_imag, turn_sin * diff_real + turn_cos * diff_imag]
    )
    return jnp.where(upper, turned, spectrum + partner)


def complex_turn(apply_matrix, spectrum, mat_cos, mat_sin, inverse):
    real_part, imag_part = (spectrum[0], spectrum[1])
    sign = 1.0 if inverse else -1.0
    return jnp.stack(
        [
            apply_matrix(mat_cos, real_part) - sign * apply_matrix(mat_sin, imag_part),
            apply_matrix(mat_cos, imag_part) + sign * apply_matrix(mat_sin, real_part),
        ]
    )


def transform_rows(spectrum, mat_cos, mat_sin, inverse):

    def apply_matrix(matrix, values):
        return jnp.einsum("sm,myz->syz", matrix, values, precision=HIGH)

    return complex_turn(apply_matrix, spectrum, mat_cos, mat_sin, inverse)


def transform_columns(spectrum, mat_cos, mat_sin, inverse):

    def apply_matrix(matrix, values):
        return jnp.einsum("sm,xmz->xsz", matrix, values, precision=HIGH)

    return complex_turn(apply_matrix, spectrum, mat_cos, mat_sin, inverse)


def complex_block(mat_cos, mat_sin, inverse):
    turn_imag = mat_sin if inverse else -mat_sin
    return jnp.stack([jnp.stack([mat_cos, -turn_imag]), jnp.stack([turn_imag, mat_cos])])


def place_table(base, values, span):
    atoms_count = base.shape[0]
    slots_index = jnp.arange(span, dtype=jnp.int32)[:, None]
    table = jnp.zeros((span, atoms_count), jnp.float32)
    for k in range(6):
        table = table + jnp.where(slots_index == (base + k)[None, :], values[k][None, :], 0.0)
    return table


def place_depth(base, values, extent):
    depth_index = jnp.arange(extent, dtype=jnp.int32)[None, :]
    table = jnp.zeros((base.shape[0], extent), jnp.float32)
    for k in range(6):
        table = table + jnp.where(
            depth_index == ((base + k) % extent)[:, None], values[k][:, None], 0.0
        )
    return table


def per_device(fractions, charge, cell_index, destination, live_blocks):
    rows_dev = lax.axis_size("px")
    cols_dev = lax.axis_size("py")
    span_x = K // rows_dev
    span_y = K // cols_dev
    blocks = charge.shape[0]
    width = charge.shape[1]
    capacity = max(2, 3 * blocks // (2 * cols_dev))
    slots = cols_dev * capacity
    alive = (jnp.arange(blocks, dtype=jnp.int32) < live_blocks[0]).astype(jnp.float32)
    target = destination[:, 0]
    matches = (target[:, None] == jnp.arange(cols_dev, dtype=jnp.int32)[None, :]).astype(jnp.int32)
    earlier = jnp.cumsum(matches, axis=0) - matches
    position = jnp.sum(earlier * matches, axis=1)
    slot_of = target * capacity + position
    picked = (slot_of[None, :] == jnp.arange(slots, dtype=jnp.int32)[:, None]).astype(jnp.int32)
    source_block = jnp.sum(picked * jnp.arange(blocks, dtype=jnp.int32)[None, :], axis=1)
    used = jnp.sum(picked, axis=1).astype(jnp.float32)
    payload = jnp.concatenate(
        [
            fractions,
            (charge * alive[:, None])[:, None, :],
            cell_index.astype(jnp.float32)[:, None, :],
        ],
        axis=1,
    )
    outgoing = (jnp.take(payload, source_block, axis=0) * used[:, None, None]).reshape(
        cols_dev, capacity, 5, width
    )
    arrived = lax.all_to_all(outgoing, "py", split_axis=0, concat_axis=0, tiled=True)
    atoms = slots * width
    placed = arrived.reshape(slots, 5, width).transpose(1, 0, 2).reshape(5, atoms)
    cell_value = placed[4].astype(jnp.int32)
    amounts = placed[3]
    base_x = cell_value // (span_y * K)
    base_y = cell_value // K % span_y
    base_z = cell_value % K
    splines_x, slopes_x = spline_six(placed[0])
    splines_y, slopes_y = spline_six(placed[1])
    splines_z, slopes_z = spline_six(placed[2])
    table_x = place_table(base_x, splines_x, span_x + 5)
    slope_x = place_table(base_x, slopes_x, span_x + 5)
    pad_y = -(-(span_y + 5) // 8) * 8
    table_y = place_table(base_y, splines_y, pad_y)
    slope_y = place_table(base_y, slopes_y, pad_y)
    both_z = place_depth(
        jnp.concatenate([base_z, base_z]),
        [jnp.concatenate([splines_z[k], slopes_z[k]]) for k in range(6)],
        K,
    )
    both_z = lax.optimization_barrier(both_z)
    outer_table = ((table_x * amounts[None, :])[:, None, :] * table_y[None, :, :]).reshape(-1, atoms)
    extended = jnp.dot(outer_table, both_z[:atoms], precision=HIGH)
    extended = extended.reshape(span_x + 5, pad_y, K)
    moved_rows = from_behind(extended[span_x:, :span_y], "px", 1)
    moved_cols = from_behind(extended[:span_x, span_y : span_y + 5], "py", 1)
    moved_corner = from_corner(extended[span_x:, span_y : span_y + 5], 1)
    charge_grid = extended[:span_x, :span_y]
    charge_grid = charge_grid.at[:5].add(moved_rows)
    charge_grid = charge_grid.at[:, :5].add(moved_cols)
    charge_grid = charge_grid.at[:5, :5].add(moved_corner)
    index_x = lax.axis_index("px")
    index_y = lax.axis_index("py")
    span_ky = K // rows_dev
    span_kz = K // cols_dev
    wave_cos, wave_sin = wave_tables(K)
    ahead_z = jnp.stack([wave_cos, -wave_sin]).reshape(2, cols_dev, span_kz, K)
    flat_grid = charge_grid.reshape(span_x * span_y, K)
    spectrum = jnp.einsum("cjkz,mz->jckm", ahead_z, flat_grid, precision=HIGH)
    spectrum = lax.all_to_all(spectrum, "py", 0, 0, tiled=True)
    spectrum = spectrum.reshape(cols_dev, 2, span_kz, span_x, span_y)
    turn_y = complex_block(wave_cos, wave_sin, False).reshape(2, 2, rows_dev, span_ky, cols_dev, span_y)
    spectrum = jnp.einsum("dcilsy,sckxy->idlkx", turn_y, spectrum, precision=HIGH)
    spectrum = spectrum.reshape(rows_dev, 2, span_ky, span_kz * span_x)
    spectrum = lax.all_to_all(spectrum, "px", 0, 0, tiled=True)
    spectrum = spectrum.reshape(rows_dev, 2, span_ky, span_kz, span_x)
    turn_x = complex_block(wave_cos, wave_sin, False).reshape(2, 2, K, rows_dev, span_x)
    spectrum = jnp.einsum("dcqrx,rclkx->qdlk", turn_x, spectrum, precision=HIGH)
    wave_x = jnp.arange(K, dtype=jnp.int32)
    wave_y = index_x * span_ky + jnp.arange(span_ky, dtype=jnp.int32)
    wave_z = index_y * span_kz + jnp.arange(span_kz, dtype=jnp.int32)
    kernel = influence(wave_x[:, None, None], wave_y[None, :, None], wave_z[None, None, :], K) * (
        1.0 / float(K**3)
    )
    spectrum = spectrum * kernel[:, None]
    back_x = complex_block(wave_cos, wave_sin, True).reshape(2, 2, rows_dev, span_x, K)
    spectrum = jnp.einsum("dcrxq,qclk->rdlkx", back_x, spectrum, precision=HIGH)
    spectrum = spectrum.reshape(rows_dev, 2, span_ky, span_kz * span_x)
    spectrum = lax.all_to_all(spectrum, "px", 0, 0, tiled=True)
    spectrum = spectrum.reshape(rows_dev, 2, span_ky, span_kz, span_x)
    back_y = complex_block(wave_cos, wave_sin, True).reshape(2, 2, cols_dev, span_y, rows_dev, span_ky)
    spectrum = jnp.einsum("dcsyil,iclkx->sdkxy", back_y, spectrum, precision=HIGH)
    spectrum = spectrum.reshape(cols_dev, 2, span_kz, span_x * span_y)
    spectrum = lax.all_to_all(spectrum, "py", 0, 0, tiled=True)
    back_z = jnp.stack([wave_cos, -wave_sin], axis=1).reshape(K, 2, cols_dev, span_kz)
    potential = jnp.einsum("zcjk,jckm->mz", back_z, spectrum, precision=HIGH)
    potential = potential.reshape(span_x, span_y, K)
    lower_rows = from_behind(potential[:5], "px", -1)
    potential = jnp.concatenate([potential, lower_rows], axis=0)
    lower_cols = from_behind(potential[:, :5], "py", -1)
    gap = jnp.zeros((span_x + 5, pad_y - span_y - 5, K), jnp.float32)
    potential = jnp.concatenate([potential, lower_cols, gap], axis=1).reshape(-1, K)

    sampled = lax.dot_general(
        potential, both_z, (((1,), (1,)), ((), ())), precision=HIGH
    ).reshape(span_x + 5, pad_y, 2, atoms)
    plain = sampled[:, :, 0]
    sloped = sampled[:, :, 1]
    force_x = jnp.sum(slope_x[:, None, :] * table_y[None, :, :] * plain, axis=(0, 1))
    force_y = jnp.sum(table_x[:, None, :] * slope_y[None, :, :] * plain, axis=(0, 1))
    force_z = jnp.sum(table_x[:, None, :] * table_y[None, :, :] * sloped, axis=(0, 1))
    pulled = (-amounts[None, :] * jnp.stack([force_x, force_y, force_z])).reshape(3, slots, width)
    pulled = pulled.transpose(1, 0, 2).reshape(cols_dev, capacity, 3, width)
    returned = lax.all_to_all(pulled, "py", split_axis=0, concat_axis=0, tiled=True).reshape(
        slots, 3, width
    )
    return jnp.take(returned, slot_of, axis=0) * alive[:, None, None]


def solution(mesh):
    placed = (
        P(("px", "py"), None, None),
        P(("px", "py"), None),
        P(("px", "py"), None),
        P(("px", "py"), None),
        P(("px", "py")),
    )
    return jax.shard_map(
        per_device,
        mesh=mesh,
        in_specs=placed,
        out_specs=P(("px", "py"), None, None),
        check_vma=False,
    )
```

```python
import math

import jax
import jax.numpy as jnp
from jax import lax
from jax.sharding import PartitionSpec as P

K = 256


EWALD_GAIN = 4.0
EWALD_BETA = 0.6
SPLINE_SUMS = (1.0 / 120.0, 26.0 / 120.0, 66.0 / 120.0, 26.0 / 120.0, 1.0 / 120.0)
HIGHEST = lax.Precision.HIGHEST
HIGH = lax.Precision.HIGH


def swapped(block, axis, bit):
    count = lax.axis_size(axis)
    route = []
    for low in range(count):
        high = low | 1 << bit
        if high != low and high < count:
            route += [(low, high), (high, low)]
    return lax.ppermute(block, axis, route)


def from_behind(value, axis, steps):
    count = lax.axis_size(axis)
    pairs = [(source, (source + steps) % count) for source in range(count)]
    return lax.ppermute(value, axis, pairs)


def from_corner(value, steps):
    rows = lax.axis_size("px")
    cols = lax.axis_size("py")
    pairs = [
        (i * cols + j, (i + steps) % rows * cols + (j + steps) % cols)
        for i in range(rows)
        for j in range(cols)
    ]
    return lax.ppermute(value, ("px", "py"), pairs)


def spline_six(u):
    older_values = [1.0 - u, u]
    slopes = []
    for spline_order in range(3, 7):
        newer_values = []
        for k in range(spline_order):
            from_left = older_values[k - 1] if k >= 1 else jnp.zeros_like(u)
            from_right = older_values[k] if k <= spline_order - 2 else jnp.zeros_like(u)
            newer_values.append(
                ((u + (spline_order - 1 - k)) * from_left + (k + 1 - u) * from_right)
                * (1.0 / (spline_order - 1))
            )
        if spline_order == 6:
            slopes = [
                (older_values[k - 1] if k >= 1 else jnp.zeros_like(u))
                - (older_values[k] if k <= 4 else jnp.zeros_like(u))
                for k in range(6)
            ]
        older_values = newer_values
    return (older_values, slopes)


def modulus(wave, extent):
    cos_sum = jnp.zeros(wave.shape, jnp.float32)
    sin_sum = jnp.zeros(wave.shape, jnp.float32)
    for j, value in enumerate(SPLINE_SUMS):
        angle = 2.0 * math.pi / extent * (wave * j % extent).astype(jnp.float32)
        cos_sum = cos_sum + value * jnp.cos(angle)
        sin_sum = sin_sum + value * jnp.sin(angle)
    return 1.0 / (cos_sum * cos_sum + sin_sum * sin_sum)


def influence(wave_x, wave_y, wave_z, extent):
    folded_x = jnp.where(2 * wave_x < extent, wave_x, wave_x - extent).astype(jnp.float32) / extent
    folded_y = jnp.where(2 * wave_y < extent, wave_y, wave_y - extent).astype(jnp.float32) / extent
    folded_z = jnp.where(2 * wave_z < extent, wave_z, wave_z - extent).astype(jnp.float32) / extent
    squared = folded_x * folded_x + folded_y * folded_y + folded_z * folded_z
    safe_squared = jnp.where(squared > 0, squared, 1.0)
    value = (
        EWALD_GAIN
        * jnp.exp(-(math.pi * math.pi) * squared / (EWALD_BETA * EWALD_BETA))
        / safe_squared
    )
    value = value * modulus(wave_x, extent) * modulus(wave_y, extent) * modulus(wave_z, extent)
    return jnp.where(squared > 0, value, 0.0)


def wave_tables(extent):
    steps = jnp.arange(extent, dtype=jnp.int32)
    product = steps[:, None] * steps[None, :] % extent
    angle = 2.0 * math.pi / extent * product.astype(jnp.float32)
    return (jnp.cos(angle), jnp.sin(angle))


def local_forward(start, count, parts):
    outputs = jnp.arange(count, dtype=jnp.int32)[:, None]
    inputs = jnp.arange(count, dtype=jnp.int32)[None, :]
    total = parts * count
    product = inputs * (start + parts * outputs) % total
    angle = -2.0 * math.pi / total * product.astype(jnp.float32)
    return (jnp.cos(angle), jnp.sin(angle))


def reverse_bits(index, count_bits):
    result = jnp.zeros((), jnp.int32)
    for b in range(count_bits):
        result = result + ((index >> b & 1) << count_bits - 1 - b)
    return result


def mix_rows(spectrum, mat_cos, mat_sin):

    def apply_matrix(matrix, values):
        return jnp.einsum("sm,myz->syz", matrix, values, precision=HIGH)

    real_part, imag_part = (spectrum[0], spectrum[1])
    return jnp.stack(
        [
            apply_matrix(mat_cos, real_part) - apply_matrix(mat_sin, imag_part),
            apply_matrix(mat_cos, imag_part) + apply_matrix(mat_sin, real_part),
        ]
    )


def mix_columns(spectrum, mat_cos, mat_sin):

    def apply_matrix(matrix, values):
        return jnp.einsum("sm,xmz->xsz", matrix, values, precision=HIGH)

    real_part, imag_part = (spectrum[0], spectrum[1])
    return jnp.stack(
        [
            apply_matrix(mat_cos, real_part) - apply_matrix(mat_sin, imag_part),
            apply_matrix(mat_cos, imag_part) + apply_matrix(mat_sin, real_part),
        ]
    )


def swap_rows(spectrum, bit_number):
    return swapped(spectrum, "px", bit_number)


def swap_columns(spectrum, bit_number):
    return swapped(spectrum, "py", bit_number)


def butterfly_section(spectrum, index, bit_number, inverse, exchanger):
    upper = index >> bit_number & 1 == 1
    lower = (index & (1 << bit_number) - 1).astype(jnp.float32)
    angle = -2.0 * math.pi / 2 ** (bit_number + 1) * lower
    turn_cos = jnp.cos(angle)
    turn_sin = jnp.sin(angle)
    real_part, imag_part = (spectrum[0], spectrum[1])
    if inverse:
        turned = jnp.stack(
            [
                turn_cos * real_part + turn_sin * imag_part,
                turn_cos * imag_part - turn_sin * real_part,
            ]
        )
        own_value = jnp.where(upper, turned, spectrum)
        partner = exchanger(own_value, bit_number)
        return jnp.where(upper, partner - own_value, own_value + partner)
    partner = exchanger(spectrum, bit_number)
    diff_real = partner[0] - real_part
    diff_imag = partner[1] - imag_part
    turned = jnp.stack(
        [turn_cos * diff_real - turn_sin * diff_imag, turn_sin * diff_real + turn_cos * diff_imag]
    )
    return jnp.where(upper, turned, spectrum + partner)


def complex_turn(apply_matrix, spectrum, mat_cos, mat_sin, inverse):
    real_part, imag_part = (spectrum[0], spectrum[1])
    sign = 1.0 if inverse else -1.0
    return jnp.stack(
        [
            apply_matrix(mat_cos, real_part) - sign * apply_matrix(mat_sin, imag_part),
            apply_matrix(mat_cos, imag_part) + sign * apply_matrix(mat_sin, real_part),
        ]
    )


def transform_rows(spectrum, mat_cos, mat_sin, inverse):

    def apply_matrix(matrix, values):
        return jnp.einsum("sm,myz->syz", matrix, values, precision=HIGH)

    return complex_turn(apply_matrix, spectrum, mat_cos, mat_sin, inverse)


def transform_columns(spectrum, mat_cos, mat_sin, inverse):

    def apply_matrix(matrix, values):
        return jnp.einsum("sm,xmz->xsz", matrix, values, precision=HIGH)

    return complex_turn(apply_matrix, spectrum, mat_cos, mat_sin, inverse)


def complex_block(mat_cos, mat_sin, inverse):
    turn_imag = mat_sin if inverse else -mat_sin
    return jnp.stack([jnp.stack([mat_cos, -turn_imag]), jnp.stack([turn_imag, mat_cos])])


def place_table(base, values, span):
    atoms_count = base.shape[0]
    slots_index = jnp.arange(span, dtype=jnp.int32)[:, None]
    table = jnp.zeros((span, atoms_count), jnp.float32)
    for k in range(6):
        table = table + jnp.where(slots_index == (base + k)[None, :], values[k][None, :], 0.0)
    return table


def place_depth(base, values, extent):
    depth_index = jnp.arange(extent, dtype=jnp.int32)[None, :]
    table = jnp.zeros((base.shape[0], extent), jnp.float32)
    for k in range(6):
        table = table + jnp.where(
            depth_index == ((base + k) % extent)[:, None], values[k][:, None], 0.0
        )
    return table


def per_device(fractions, charge, cell_index, destination, live_blocks):
    rows_dev = lax.axis_size("px")
    cols_dev = lax.axis_size("py")
    span_x = K // rows_dev
    span_y = K // cols_dev
    blocks = charge.shape[0]
    width = charge.shape[1]
    capacity = max(2, 3 * blocks // (2 * cols_dev))
    slots = cols_dev * capacity
    alive = (jnp.arange(blocks, dtype=jnp.int32) < live_blocks[0]).astype(jnp.float32)
    target = destination[:, 0]
    matches = (target[:, None] == jnp.arange(cols_dev, dtype=jnp.int32)[None, :]).astype(jnp.int32)
    earlier = jnp.cumsum(matches, axis=0) - matches
    position = jnp.sum(earlier * matches, axis=1)
    slot_of = target * capacity + position
    picked = (slot_of[None, :] == jnp.arange(slots, dtype=jnp.int32)[:, None]).astype(jnp.int32)
    source_block = jnp.sum(picked * jnp.arange(blocks, dtype=jnp.int32)[None, :], axis=1)
    used = jnp.sum(picked, axis=1).astype(jnp.float32)
    payload = jnp.concatenate(
        [
            fractions,
            (charge * alive[:, None])[:, None, :],
            cell_index.astype(jnp.float32)[:, None, :],
        ],
        axis=1,
    )
    outgoing = (jnp.take(payload, source_block, axis=0) * used[:, None, None]).reshape(
        cols_dev, capacity, 5, width
    )
    arrived = lax.all_to_all(outgoing, "py", split_axis=0, concat_axis=0, tiled=True)
    atoms = slots * width
    placed = arrived.reshape(slots, 5, width).transpose(1, 0, 2).reshape(5, atoms)
    cell_value = placed[4].astype(jnp.int32)
    amounts = placed[3]
    base_x = cell_value // (span_y * K)
    base_y = cell_value // K % span_y
    base_z = cell_value % K
    splines_x, slopes_x = spline_six(placed[0])
    splines_y, slopes_y = spline_six(placed[1])
    splines_z, slopes_z = spline_six(placed[2])
    table_x = place_table(base_x, splines_x, span_x + 5)
    slope_x = place_table(base_x, slopes_x, span_x + 5)
    pad_y = -(-(span_y + 5) // 8) * 8
    table_y = place_table(base_y, splines_y, pad_y)
    slope_y = place_table(base_y, slopes_y, pad_y)
    table_z = place_depth(base_z, splines_z, K)
    slope_z = place_depth(base_z, slopes_z, K)
    outer_table = ((table_x * amounts[None, :])[:, None, :] * table_y[None, :, :]).reshape(-1, atoms)
    extended = jnp.dot(outer_table, table_z, precision=HIGH)
    extended = extended.reshape(span_x + 5, pad_y, K)
    moved_rows = from_behind(extended[span_x:, :span_y], "px", 1)
    moved_cols = from_behind(extended[:span_x, span_y : span_y + 5], "py", 1)
    moved_corner = from_corner(extended[span_x:, span_y : span_y + 5], 1)
    charge_grid = extended[:span_x, :span_y]
    charge_grid = charge_grid.at[:5].add(moved_rows)
    charge_grid = charge_grid.at[:, :5].add(moved_cols)
    charge_grid = charge_grid.at[:5, :5].add(moved_corner)
    index_x = lax.axis_index("px")
    index_y = lax.axis_index("py")
    span_ky = K // rows_dev
    span_kz = K // cols_dev
    wave_cos, wave_sin = wave_tables(K)
    ahead_z = jnp.stack([wave_cos, -wave_sin]).reshape(2, cols_dev, span_kz, K)
    flat_grid = charge_grid.reshape(span_x * span_y, K)
    spectrum = jnp.einsum("cjkz,mz->jckm", ahead_z, flat_grid, precision=HIGH)
    spectrum = lax.all_to_all(spectrum, "py", 0, 0, tiled=True)
    spectrum = spectrum.reshape(cols_dev, 2, span_kz, span_x, span_y)
    turn_y = complex_block(wave_cos, wave_sin, False).reshape(2, 2, rows_dev, span_ky, cols_dev, span_y)
    spectrum = jnp.einsum("dcilsy,sckxy->idlkx", turn_y, spectrum, precision=HIGH)
    spectrum = spectrum.reshape(rows_dev, 2, span_ky, span_kz * span_x)
    spectrum = lax.all_to_all(spectrum, "px", 0, 0, tiled=True)
    spectrum = spectrum.reshape(rows_dev, 2, span_ky, span_kz, span_x)
    turn_x = complex_block(wave_cos, wave_sin, False).reshape(2, 2, K, rows_dev, span_x)
    spectrum = jnp.einsum("dcqrx,rclkx->qdlk", turn_x, spectrum, precision=HIGH)
    wave_x = jnp.arange(K, dtype=jnp.int32)
    wave_y = index_x * span_ky + jnp.arange(span_ky, dtype=jnp.int32)
    wave_z = index_y * span_kz + jnp.arange(span_kz, dtype=jnp.int32)
    kernel = influence(wave_x[:, None, None], wave_y[None, :, None], wave_z[None, None, :], K) * (
        1.0 / float(K**3)
    )
    spectrum = spectrum * kernel[:, None]
    back_x = complex_block(wave_cos, wave_sin, True).reshape(2, 2, rows_dev, span_x, K)
    spectrum = jnp.einsum("dcrxq,qclk->rdlkx", back_x, spectrum, precision=HIGH)
    spectrum = spectrum.reshape(rows_dev, 2, span_ky, span_kz * span_x)
    spectrum = lax.all_to_all(spectrum, "px", 0, 0, tiled=True)
    spectrum = spectrum.reshape(rows_dev, 2, span_ky, span_kz, span_x)
    back_y = complex_block(wave_cos, wave_sin, True).reshape(2, 2, cols_dev, span_y, rows_dev, span_ky)
    spectrum = jnp.einsum("dcsyil,iclkx->sdkxy", back_y, spectrum, precision=HIGH)
    spectrum = spectrum.reshape(cols_dev, 2, span_kz, span_x * span_y)
    spectrum = lax.all_to_all(spectrum, "py", 0, 0, tiled=True)
    back_z = jnp.stack([wave_cos, -wave_sin], axis=1).reshape(K, 2, cols_dev, span_kz)
    potential = jnp.einsum("zcjk,jckm->mz", back_z, spectrum, precision=HIGH)
    potential = potential.reshape(span_x, span_y, K)
    lower_rows = from_behind(potential[:5], "px", -1)
    potential = jnp.concatenate([potential, lower_rows], axis=0)
    lower_cols = from_behind(potential[:, :5], "py", -1)
    gap = jnp.zeros((span_x + 5, pad_y - span_y - 5, K), jnp.float32)
    potential = jnp.concatenate([potential, lower_cols, gap], axis=1).reshape(-1, K)

    both_z = jnp.concatenate([table_z, slope_z], axis=0)
    sampled = lax.dot_general(
        potential, both_z, (((1,), (1,)), ((), ())), precision=HIGH
    ).reshape(span_x + 5, pad_y, 2, atoms)
    plain = sampled[:, :, 0]
    sloped = sampled[:, :, 1]
    force_x = jnp.sum(slope_x[:, None, :] * table_y[None, :, :] * plain, axis=(0, 1))
    force_y = jnp.sum(table_x[:, None, :] * slope_y[None, :, :] * plain, axis=(0, 1))
    force_z = jnp.sum(table_x[:, None, :] * table_y[None, :, :] * sloped, axis=(0, 1))
    pulled = (-amounts[None, :] * jnp.stack([force_x, force_y, force_z])).reshape(3, slots, width)
    pulled = pulled.transpose(1, 0, 2).reshape(cols_dev, capacity, 3, width)
    returned = lax.all_to_all(pulled, "py", split_axis=0, concat_axis=0, tiled=True).reshape(
        slots, 3, width
    )
    return jnp.take(returned, slot_of, axis=0) * alive[:, None, None]


def solution(mesh):
    placed = (
        P(("px", "py"), None, None),
        P(("px", "py"), None),
        P(("px", "py"), None),
        P(("px", "py"), None),
        P(("px", "py")),
    )
    return jax.shard_map(
        per_device,
        mesh=mesh,
        in_specs=placed,
        out_specs=P(("px", "py"), None, None),
        check_vma=False,
    )
```

```python
import math

import jax
import jax.numpy as jnp
from jax import lax
from jax.sharding import PartitionSpec as P

K = 256


EWALD_GAIN = 4.0
EWALD_BETA = 0.6
SPLINE_SUMS = (1.0 / 120.0, 26.0 / 120.0, 66.0 / 120.0, 26.0 / 120.0, 1.0 / 120.0)
HIGHEST = lax.Precision.HIGHEST
HIGH = lax.Precision.HIGH


def swapped(block, axis, bit):
    count = lax.axis_size(axis)
    route = []
    for low in range(count):
        high = low | 1 << bit
        if high != low and high < count:
            route += [(low, high), (high, low)]
    return lax.ppermute(block, axis, route)


def from_behind(value, axis, steps):
    count = lax.axis_size(axis)
    pairs = [(source, (source + steps) % count) for source in range(count)]
    return lax.ppermute(value, axis, pairs)


def from_corner(value, steps):
    rows = lax.axis_size("px")
    cols = lax.axis_size("py")
    pairs = [
        (i * cols + j, (i + steps) % rows * cols + (j + steps) % cols)
        for i in range(rows)
        for j in range(cols)
    ]
    return lax.ppermute(value, ("px", "py"), pairs)


def spline_six(u):
    older_values = [1.0 - u, u]
    slopes = []
    for spline_order in range(3, 7):
        newer_values = []
        for k in range(spline_order):
            from_left = older_values[k - 1] if k >= 1 else jnp.zeros_like(u)
            from_right = older_values[k] if k <= spline_order - 2 else jnp.zeros_like(u)
            newer_values.append(
                ((u + (spline_order - 1 - k)) * from_left + (k + 1 - u) * from_right)
                * (1.0 / (spline_order - 1))
            )
        if spline_order == 6:
            slopes = [
                (older_values[k - 1] if k >= 1 else jnp.zeros_like(u))
                - (older_values[k] if k <= 4 else jnp.zeros_like(u))
                for k in range(6)
            ]
        older_values = newer_values
    return (older_values, slopes)


def modulus(wave, extent):
    cos_sum = jnp.zeros(wave.shape, jnp.float32)
    sin_sum = jnp.zeros(wave.shape, jnp.float32)
    for j, value in enumerate(SPLINE_SUMS):
        angle = 2.0 * math.pi / extent * (wave * j % extent).astype(jnp.float32)
        cos_sum = cos_sum + value * jnp.cos(angle)
        sin_sum = sin_sum + value * jnp.sin(angle)
    return 1.0 / (cos_sum * cos_sum + sin_sum * sin_sum)


def influence(wave_x, wave_y, wave_z, extent):
    folded_x = jnp.where(2 * wave_x < extent, wave_x, wave_x - extent).astype(jnp.float32) / extent
    folded_y = jnp.where(2 * wave_y < extent, wave_y, wave_y - extent).astype(jnp.float32) / extent
    folded_z = jnp.where(2 * wave_z < extent, wave_z, wave_z - extent).astype(jnp.float32) / extent
    squared = folded_x * folded_x + folded_y * folded_y + folded_z * folded_z
    safe_squared = jnp.where(squared > 0, squared, 1.0)
    value = (
        EWALD_GAIN
        * jnp.exp(-(math.pi * math.pi) * squared / (EWALD_BETA * EWALD_BETA))
        / safe_squared
    )
    value = value * modulus(wave_x, extent) * modulus(wave_y, extent) * modulus(wave_z, extent)
    return jnp.where(squared > 0, value, 0.0)


def wave_tables(extent):
    steps = jnp.arange(extent, dtype=jnp.int32)
    product = steps[:, None] * steps[None, :] % extent
    angle = 2.0 * math.pi / extent * product.astype(jnp.float32)
    return (jnp.cos(angle), jnp.sin(angle))


def local_forward(start, count, parts):
    outputs = jnp.arange(count, dtype=jnp.int32)[:, None]
    inputs = jnp.arange(count, dtype=jnp.int32)[None, :]
    total = parts * count
    product = inputs * (start + parts * outputs) % total
    angle = -2.0 * math.pi / total * product.astype(jnp.float32)
    return (jnp.cos(angle), jnp.sin(angle))


def reverse_bits(index, count_bits):
    result = jnp.zeros((), jnp.int32)
    for b in range(count_bits):
        result = result + ((index >> b & 1) << count_bits - 1 - b)
    return result


def mix_rows(spectrum, mat_cos, mat_sin):

    def apply_matrix(matrix, values):
        return jnp.einsum("sm,myz->syz", matrix, values, precision=HIGH)

    real_part, imag_part = (spectrum[0], spectrum[1])
    return jnp.stack(
        [
            apply_matrix(mat_cos, real_part) - apply_matrix(mat_sin, imag_part),
            apply_matrix(mat_cos, imag_part) + apply_matrix(mat_sin, real_part),
        ]
    )


def mix_columns(spectrum, mat_cos, mat_sin):

    def apply_matrix(matrix, values):
        return jnp.einsum("sm,xmz->xsz", matrix, values, precision=HIGH)

    real_part, imag_part = (spectrum[0], spectrum[1])
    return jnp.stack(
        [
            apply_matrix(mat_cos, real_part) - apply_matrix(mat_sin, imag_part),
            apply_matrix(mat_cos, imag_part) + apply_matrix(mat_sin, real_part),
        ]
    )


def swap_rows(spectrum, bit_number):
    return swapped(spectrum, "px", bit_number)


def swap_columns(spectrum, bit_number):
    return swapped(spectrum, "py", bit_number)


def butterfly_section(spectrum, index, bit_number, inverse, exchanger):
    upper = index >> bit_number & 1 == 1
    lower = (index & (1 << bit_number) - 1).astype(jnp.float32)
    angle = -2.0 * math.pi / 2 ** (bit_number + 1) * lower
    turn_cos = jnp.cos(angle)
    turn_sin = jnp.sin(angle)
    real_part, imag_part = (spectrum[0], spectrum[1])
    if inverse:
        turned = jnp.stack(
            [
                turn_cos * real_part + turn_sin * imag_part,
                turn_cos * imag_part - turn_sin * real_part,
            ]
        )
        own_value = jnp.where(upper, turned, spectrum)
        partner = exchanger(own_value, bit_number)
        return jnp.where(upper, partner - own_value, own_value + partner)
    partner = exchanger(spectrum, bit_number)
    diff_real = partner[0] - real_part
    diff_imag = partner[1] - imag_part
    turned = jnp.stack(
        [turn_cos * diff_real - turn_sin * diff_imag, turn_sin * diff_real + turn_cos * diff_imag]
    )
    return jnp.where(upper, turned, spectrum + partner)


def complex_turn(apply_matrix, spectrum, mat_cos, mat_sin, inverse):
    real_part, imag_part = (spectrum[0], spectrum[1])
    sign = 1.0 if inverse else -1.0
    return jnp.stack(
        [
            apply_matrix(mat_cos, real_part) - sign * apply_matrix(mat_sin, imag_part),
            apply_matrix(mat_cos, imag_part) + sign * apply_matrix(mat_sin, real_part),
        ]
    )


def transform_rows(spectrum, mat_cos, mat_sin, inverse):

    def apply_matrix(matrix, values):
        return jnp.einsum("sm,myz->syz", matrix, values, precision=HIGH)

    return complex_turn(apply_matrix, spectrum, mat_cos, mat_sin, inverse)


def transform_columns(spectrum, mat_cos, mat_sin, inverse):

    def apply_matrix(matrix, values):
        return jnp.einsum("sm,xmz->xsz", matrix, values, precision=HIGH)

    return complex_turn(apply_matrix, spectrum, mat_cos, mat_sin, inverse)


def complex_block(mat_cos, mat_sin, inverse):
    turn_imag = mat_sin if inverse else -mat_sin
    return jnp.stack([jnp.stack([mat_cos, -turn_imag]), jnp.stack([turn_imag, mat_cos])])


def place_table(base, values, span):
    atoms_count = base.shape[0]
    slots_index = jnp.arange(span, dtype=jnp.int32)[:, None]
    table = jnp.zeros((span, atoms_count), jnp.float32)
    for k in range(6):
        table = table + jnp.where(slots_index == (base + k)[None, :], values[k][None, :], 0.0)
    return table


def place_depth(base, values, extent):
    depth_index = jnp.arange(extent, dtype=jnp.int32)[None, :]
    table = jnp.zeros((base.shape[0], extent), jnp.float32)
    for k in range(6):
        table = table + jnp.where(
            depth_index == ((base + k) % extent)[:, None], values[k][:, None], 0.0
        )
    return table


def per_device(fractions, charge, cell_index, destination, live_blocks):
    rows_dev = lax.axis_size("px")
    cols_dev = lax.axis_size("py")
    span_x = K // rows_dev
    span_y = K // cols_dev
    blocks = charge.shape[0]
    width = charge.shape[1]
    capacity = max(2, 3 * blocks // (2 * cols_dev))
    slots = cols_dev * capacity
    alive = (jnp.arange(blocks, dtype=jnp.int32) < live_blocks[0]).astype(jnp.float32)
    target = destination[:, 0]
    matches = (target[:, None] == jnp.arange(cols_dev, dtype=jnp.int32)[None, :]).astype(jnp.int32)
    earlier = jnp.cumsum(matches, axis=0) - matches
    position = jnp.sum(earlier * matches, axis=1)
    slot_of = target * capacity + position
    picked = (slot_of[None, :] == jnp.arange(slots, dtype=jnp.int32)[:, None]).astype(jnp.int32)
    source_block = jnp.sum(picked * jnp.arange(blocks, dtype=jnp.int32)[None, :], axis=1)
    used = jnp.sum(picked, axis=1).astype(jnp.float32)
    payload = jnp.concatenate(
        [
            fractions,
            (charge * alive[:, None])[:, None, :],
            cell_index.astype(jnp.float32)[:, None, :],
        ],
        axis=1,
    )
    outgoing = (jnp.take(payload, source_block, axis=0) * used[:, None, None]).reshape(
        cols_dev, capacity, 5, width
    )
    arrived = lax.all_to_all(outgoing, "py", split_axis=0, concat_axis=0, tiled=True)
    atoms = slots * width
    placed = arrived.reshape(slots, 5, width).transpose(1, 0, 2).reshape(5, atoms)
    cell_value = placed[4].astype(jnp.int32)
    amounts = placed[3]
    base_x = cell_value // (span_y * K)
    base_y = cell_value // K % span_y
    base_z = cell_value % K
    splines_x, slopes_x = spline_six(placed[0])
    splines_y, slopes_y = spline_six(placed[1])
    splines_z, slopes_z = spline_six(placed[2])
    table_x = place_table(base_x, splines_x, span_x + 5)
    slope_x = place_table(base_x, slopes_x, span_x + 5)
    pad_y = -(-(span_y + 5) // 8) * 8
    table_y = place_table(base_y, splines_y, pad_y)
    slope_y = place_table(base_y, slopes_y, pad_y)
    table_z = place_depth(base_z, splines_z, K)
    slope_z = place_depth(base_z, slopes_z, K)
    outer_table = ((table_x * amounts[None, :])[:, None, :] * table_y[None, :, :]).reshape(-1, atoms)
    extended = jnp.dot(outer_table, lax.optimization_barrier(table_z), precision=HIGH)
    extended = extended.reshape(span_x + 5, pad_y, K)
    moved_rows = from_behind(extended[span_x:, :span_y], "px", 1)
    moved_cols = from_behind(extended[:span_x, span_y : span_y + 5], "py", 1)
    moved_corner = from_corner(extended[span_x:, span_y : span_y + 5], 1)
    charge_grid = extended[:span_x, :span_y]
    charge_grid = charge_grid.at[:5].add(moved_rows)
    charge_grid = charge_grid.at[:, :5].add(moved_cols)
    charge_grid = charge_grid.at[:5, :5].add(moved_corner)
    index_x = lax.axis_index("px")
    index_y = lax.axis_index("py")
    span_ky = K // rows_dev
    span_kz = K // cols_dev
    wave_cos, wave_sin = wave_tables(K)
    ahead_z = jnp.stack([wave_cos, -wave_sin]).reshape(2, cols_dev, span_kz, K)
    flat_grid = charge_grid.reshape(span_x * span_y, K)
    spectrum = jnp.einsum("cjkz,mz->jckm", ahead_z, flat_grid, precision=HIGH)
    spectrum = lax.all_to_all(spectrum, "py", 0, 0, tiled=True)
    spectrum = spectrum.reshape(cols_dev, 2, span_kz, span_x, span_y)
    turn_y = complex_block(wave_cos, wave_sin, False).reshape(2, 2, rows_dev, span_ky, cols_dev, span_y)
    spectrum = jnp.einsum("dcilsy,sckxy->idlkx", turn_y, spectrum, precision=HIGH)
    spectrum = spectrum.reshape(rows_dev, 2, span_ky, span_kz * span_x)
    spectrum = lax.all_to_all(spectrum, "px", 0, 0, tiled=True)
    spectrum = spectrum.reshape(rows_dev, 2, span_ky, span_kz, span_x)
    turn_x = complex_block(wave_cos, wave_sin, False).reshape(2, 2, K, rows_dev, span_x)
    spectrum = jnp.einsum("dcqrx,rclkx->qdlk", turn_x, spectrum, precision=HIGH)
    wave_x = jnp.arange(K, dtype=jnp.int32)
    wave_y = index_x * span_ky + jnp.arange(span_ky, dtype=jnp.int32)
    wave_z = index_y * span_kz + jnp.arange(span_kz, dtype=jnp.int32)
    kernel = influence(wave_x[:, None, None], wave_y[None, :, None], wave_z[None, None, :], K) * (
        1.0 / float(K**3)
    )
    spectrum = spectrum * kernel[:, None]
    back_x = complex_block(wave_cos, wave_sin, True).reshape(2, 2, rows_dev, span_x, K)
    spectrum = jnp.einsum("dcrxq,qclk->rdlkx", back_x, spectrum, precision=HIGH)
    spectrum = spectrum.reshape(rows_dev, 2, span_ky, span_kz * span_x)
    spectrum = lax.all_to_all(spectrum, "px", 0, 0, tiled=True)
    spectrum = spectrum.reshape(rows_dev, 2, span_ky, span_kz, span_x)
    back_y = complex_block(wave_cos, wave_sin, True).reshape(2, 2, cols_dev, span_y, rows_dev, span_ky)
    spectrum = jnp.einsum("dcsyil,iclkx->sdkxy", back_y, spectrum, precision=HIGH)
    spectrum = spectrum.reshape(cols_dev, 2, span_kz, span_x * span_y)
    spectrum = lax.all_to_all(spectrum, "py", 0, 0, tiled=True)
    back_z = jnp.stack([wave_cos, -wave_sin], axis=1).reshape(K, 2, cols_dev, span_kz)
    potential = jnp.einsum("zcjk,jckm->mz", back_z, spectrum, precision=HIGH)
    potential = potential.reshape(span_x, span_y, K)
    lower_rows = from_behind(potential[:5], "px", -1)
    potential = jnp.concatenate([potential, lower_rows], axis=0)
    lower_cols = from_behind(potential[:, :5], "py", -1)
    gap = jnp.zeros((span_x + 5, pad_y - span_y - 5, K), jnp.float32)
    potential = jnp.concatenate([potential, lower_cols, gap], axis=1).reshape(-1, K)

    late_base, late_splines, late_slopes = lax.optimization_barrier((base_z, splines_z, slopes_z))
    both_z = jnp.concatenate(
        [place_depth(late_base, late_splines, K), place_depth(late_base, late_slopes, K)], axis=0
    )
    sampled = lax.dot_general(
        potential, both_z, (((1,), (1,)), ((), ())), precision=HIGH
    ).reshape(span_x + 5, pad_y, 2, atoms)
    plain = sampled[:, :, 0]
    sloped = sampled[:, :, 1]
    force_x = jnp.sum(slope_x[:, None, :] * table_y[None, :, :] * plain, axis=(0, 1))
    force_y = jnp.sum(table_x[:, None, :] * slope_y[None, :, :] * plain, axis=(0, 1))
    force_z = jnp.sum(table_x[:, None, :] * table_y[None, :, :] * sloped, axis=(0, 1))
    pulled = (-amounts[None, :] * jnp.stack([force_x, force_y, force_z])).reshape(3, slots, width)
    pulled = pulled.transpose(1, 0, 2).reshape(cols_dev, capacity, 3, width)
    returned = lax.all_to_all(pulled, "py", split_axis=0, concat_axis=0, tiled=True).reshape(
        slots, 3, width
    )
    return jnp.take(returned, slot_of, axis=0) * alive[:, None, None]


def solution(mesh):
    placed = (
        P(("px", "py"), None, None),
        P(("px", "py"), None),
        P(("px", "py"), None),
        P(("px", "py"), None),
        P(("px", "py")),
    )
    return jax.shard_map(
        per_device,
        mesh=mesh,
        in_specs=placed,
        out_specs=P(("px", "py"), None, None),
        check_vma=False,
    )
```

```python
import math

import jax
import jax.numpy as jnp
from jax import lax
from jax.sharding import PartitionSpec as P

K = 256


EWALD_GAIN = 4.0
EWALD_BETA = 0.6
SPLINE_SUMS = (1.0 / 120.0, 26.0 / 120.0, 66.0 / 120.0, 26.0 / 120.0, 1.0 / 120.0)
HIGHEST = lax.Precision.HIGHEST
HIGH = lax.Precision.HIGH


def swapped(block, axis, bit):
    count = lax.axis_size(axis)
    route = []
    for low in range(count):
        high = low | 1 << bit
        if high != low and high < count:
            route += [(low, high), (high, low)]
    return lax.ppermute(block, axis, route)


def from_behind(value, axis, steps):
    count = lax.axis_size(axis)
    pairs = [(source, (source + steps) % count) for source in range(count)]
    return lax.ppermute(value, axis, pairs)


def from_corner(value, steps):
    rows = lax.axis_size("px")
    cols = lax.axis_size("py")
    pairs = [
        (i * cols + j, (i + steps) % rows * cols + (j + steps) % cols)
        for i in range(rows)
        for j in range(cols)
    ]
    return lax.ppermute(value, ("px", "py"), pairs)


def spline_six(u):
    older_values = [1.0 - u, u]
    slopes = []
    for spline_order in range(3, 7):
        newer_values = []
        for k in range(spline_order):
            from_left = older_values[k - 1] if k >= 1 else jnp.zeros_like(u)
            from_right = older_values[k] if k <= spline_order - 2 else jnp.zeros_like(u)
            newer_values.append(
                ((u + (spline_order - 1 - k)) * from_left + (k + 1 - u) * from_right)
                * (1.0 / (spline_order - 1))
            )
        if spline_order == 6:
            slopes = [
                (older_values[k - 1] if k >= 1 else jnp.zeros_like(u))
                - (older_values[k] if k <= 4 else jnp.zeros_like(u))
                for k in range(6)
            ]
        older_values = newer_values
    return (older_values, slopes)


def modulus(wave, extent):
    cos_sum = jnp.zeros(wave.shape, jnp.float32)
    sin_sum = jnp.zeros(wave.shape, jnp.float32)
    for j, value in enumerate(SPLINE_SUMS):
        angle = 2.0 * math.pi / extent * (wave * j % extent).astype(jnp.float32)
        cos_sum = cos_sum + value * jnp.cos(angle)
        sin_sum = sin_sum + value * jnp.sin(angle)
    return 1.0 / (cos_sum * cos_sum + sin_sum * sin_sum)


def influence(wave_x, wave_y, wave_z, extent):
    folded_x = jnp.where(2 * wave_x < extent, wave_x, wave_x - extent).astype(jnp.float32) / extent
    folded_y = jnp.where(2 * wave_y < extent, wave_y, wave_y - extent).astype(jnp.float32) / extent
    folded_z = jnp.where(2 * wave_z < extent, wave_z, wave_z - extent).astype(jnp.float32) / extent
    squared = folded_x * folded_x + folded_y * folded_y + folded_z * folded_z
    safe_squared = jnp.where(squared > 0, squared, 1.0)
    value = (
        EWALD_GAIN
        * jnp.exp(-(math.pi * math.pi) * squared / (EWALD_BETA * EWALD_BETA))
        / safe_squared
    )
    value = value * modulus(wave_x, extent) * modulus(wave_y, extent) * modulus(wave_z, extent)
    return jnp.where(squared > 0, value, 0.0)


def wave_tables(extent):
    steps = jnp.arange(extent, dtype=jnp.int32)
    product = steps[:, None] * steps[None, :] % extent
    angle = 2.0 * math.pi / extent * product.astype(jnp.float32)
    return (jnp.cos(angle), jnp.sin(angle))


def local_forward(start, count, parts):
    outputs = jnp.arange(count, dtype=jnp.int32)[:, None]
    inputs = jnp.arange(count, dtype=jnp.int32)[None, :]
    total = parts * count
    product = inputs * (start + parts * outputs) % total
    angle = -2.0 * math.pi / total * product.astype(jnp.float32)
    return (jnp.cos(angle), jnp.sin(angle))


def reverse_bits(index, count_bits):
    result = jnp.zeros((), jnp.int32)
    for b in range(count_bits):
        result = result + ((index >> b & 1) << count_bits - 1 - b)
    return result


def mix_rows(spectrum, mat_cos, mat_sin):

    def apply_matrix(matrix, values):
        return jnp.einsum("sm,myz->syz", matrix, values, precision=HIGH)

    real_part, imag_part = (spectrum[0], spectrum[1])
    return jnp.stack(
        [
            apply_matrix(mat_cos, real_part) - apply_matrix(mat_sin, imag_part),
            apply_matrix(mat_cos, imag_part) + apply_matrix(mat_sin, real_part),
        ]
    )


def mix_columns(spectrum, mat_cos, mat_sin):

    def apply_matrix(matrix, values):
        return jnp.einsum("sm,xmz->xsz", matrix, values, precision=HIGH)

    real_part, imag_part = (spectrum[0], spectrum[1])
    return jnp.stack(
        [
            apply_matrix(mat_cos, real_part) - apply_matrix(mat_sin, imag_part),
            apply_matrix(mat_cos, imag_part) + apply_matrix(mat_sin, real_part),
        ]
    )


def swap_rows(spectrum, bit_number):
    return swapped(spectrum, "px", bit_number)


def swap_columns(spectrum, bit_number):
    return swapped(spectrum, "py", bit_number)


def butterfly_section(spectrum, index, bit_number, inverse, exchanger):
    upper = index >> bit_number & 1 == 1
    lower = (index & (1 << bit_number) - 1).astype(jnp.float32)
    angle = -2.0 * math.pi / 2 ** (bit_number + 1) * lower
    turn_cos = jnp.cos(angle)
    turn_sin = jnp.sin(angle)
    real_part, imag_part = (spectrum[0], spectrum[1])
    if inverse:
        turned = jnp.stack(
            [
                turn_cos * real_part + turn_sin * imag_part,
                turn_cos * imag_part - turn_sin * real_part,
            ]
        )
        own_value = jnp.where(upper, turned, spectrum)
        partner = exchanger(own_value, bit_number)
        return jnp.where(upper, partner - own_value, own_value + partner)
    partner = exchanger(spectrum, bit_number)
    diff_real = partner[0] - real_part
    diff_imag = partner[1] - imag_part
    turned = jnp.stack(
        [turn_cos * diff_real - turn_sin * diff_imag, turn_sin * diff_real + turn_cos * diff_imag]
    )
    return jnp.where(upper, turned, spectrum + partner)


def complex_turn(apply_matrix, spectrum, mat_cos, mat_sin, inverse):
    real_part, imag_part = (spectrum[0], spectrum[1])
    sign = 1.0 if inverse else -1.0
    return jnp.stack(
        [
            apply_matrix(mat_cos, real_part) - sign * apply_matrix(mat_sin, imag_part),
            apply_matrix(mat_cos, imag_part) + sign * apply_matrix(mat_sin, real_part),
        ]
    )


def transform_rows(spectrum, mat_cos, mat_sin, inverse):

    def apply_matrix(matrix, values):
        return jnp.einsum("sm,myz->syz", matrix, values, precision=HIGH)

    return complex_turn(apply_matrix, spectrum, mat_cos, mat_sin, inverse)


def transform_columns(spectrum, mat_cos, mat_sin, inverse):

    def apply_matrix(matrix, values):
        return jnp.einsum("sm,xmz->xsz", matrix, values, precision=HIGH)

    return complex_turn(apply_matrix, spectrum, mat_cos, mat_sin, inverse)


def complex_block(mat_cos, mat_sin, inverse):
    turn_imag = mat_sin if inverse else -mat_sin
    return jnp.stack([jnp.stack([mat_cos, -turn_imag]), jnp.stack([turn_imag, mat_cos])])


def place_table(base, values, span):
    atoms_count = base.shape[0]
    slots_index = jnp.arange(span, dtype=jnp.int32)[:, None]
    table = jnp.zeros((span, atoms_count), jnp.float32)
    for k in range(6):
        table = table + jnp.where(slots_index == (base + k)[None, :], values[k][None, :], 0.0)
    return table


def place_depth(base, values, extent):
    depth_index = jnp.arange(extent, dtype=jnp.int32)[None, :]
    table = jnp.zeros((base.shape[0], extent), jnp.float32)
    for k in range(6):
        table = table + jnp.where(
            depth_index == ((base + k) % extent)[:, None], values[k][:, None], 0.0
        )
    return table


def per_device(fractions, charge, cell_index, destination, live_blocks):
    rows_dev = lax.axis_size("px")
    cols_dev = lax.axis_size("py")
    span_x = K // rows_dev
    span_y = K // cols_dev
    blocks = charge.shape[0]
    width = charge.shape[1]
    capacity = max(2, 3 * blocks // (2 * cols_dev))
    slots = cols_dev * capacity
    alive = (jnp.arange(blocks, dtype=jnp.int32) < live_blocks[0]).astype(jnp.float32)
    target = destination[:, 0]
    matches = (target[:, None] == jnp.arange(cols_dev, dtype=jnp.int32)[None, :]).astype(jnp.int32)
    earlier = jnp.cumsum(matches, axis=0) - matches
    position = jnp.sum(earlier * matches, axis=1)
    slot_of = target * capacity + position
    picked = (slot_of[None, :] == jnp.arange(slots, dtype=jnp.int32)[:, None]).astype(jnp.int32)
    source_block = jnp.sum(picked * jnp.arange(blocks, dtype=jnp.int32)[None, :], axis=1)
    used = jnp.sum(picked, axis=1).astype(jnp.float32)
    payload = jnp.concatenate(
        [
            fractions,
            (charge * alive[:, None])[:, None, :],
            cell_index.astype(jnp.float32)[:, None, :],
        ],
        axis=1,
    )
    outgoing = (jnp.take(payload, source_block, axis=0) * used[:, None, None]).reshape(
        cols_dev, capacity, 5, width
    )
    arrived = lax.all_to_all(outgoing, "py", split_axis=0, concat_axis=0, tiled=True)
    atoms = slots * width
    placed = arrived.reshape(slots, 5, width).transpose(1, 0, 2).reshape(5, atoms)
    cell_value = placed[4].astype(jnp.int32)
    amounts = placed[3]
    base_x = cell_value // (span_y * K)
    base_y = cell_value // K % span_y
    base_z = cell_value % K
    splines_x, slopes_x = spline_six(placed[0])
    splines_y, slopes_y = spline_six(placed[1])
    splines_z, slopes_z = spline_six(placed[2])
    table_x = place_table(base_x, splines_x, span_x + 5)
    slope_x = place_table(base_x, slopes_x, span_x + 5)
    pad_y = -(-(span_y + 5) // 8) * 8
    table_y = place_table(base_y, splines_y, pad_y)
    slope_y = place_table(base_y, slopes_y, pad_y)
    table_z = place_depth(base_z, splines_z, K)
    slope_z = place_depth(base_z, slopes_z, K)
    outer_table = ((table_x * amounts[None, :])[:, None, :] * table_y[None, :, :]).reshape(-1, atoms)
    table_z = lax.optimization_barrier(table_z)
    extended = jnp.dot(outer_table, table_z, precision=HIGH)
    extended = extended.reshape(span_x + 5, pad_y, K)
    moved_rows = from_behind(extended[span_x:, :span_y], "px", 1)
    moved_cols = from_behind(extended[:span_x, span_y : span_y + 5], "py", 1)
    moved_corner = from_corner(extended[span_x:, span_y : span_y + 5], 1)
    charge_grid = extended[:span_x, :span_y]
    charge_grid = charge_grid.at[:5].add(moved_rows)
    charge_grid = charge_grid.at[:, :5].add(moved_cols)
    charge_grid = charge_grid.at[:5, :5].add(moved_corner)
    index_x = lax.axis_index("px")
    index_y = lax.axis_index("py")
    span_ky = K // rows_dev
    span_kz = K // cols_dev
    wave_cos, wave_sin = wave_tables(K)
    ahead_z = jnp.stack([wave_cos, -wave_sin]).reshape(2, cols_dev, span_kz, K)
    flat_grid = charge_grid.reshape(span_x * span_y, K)
    spectrum = jnp.einsum("cjkz,mz->jckm", ahead_z, flat_grid, precision=HIGH)
    spectrum = lax.all_to_all(spectrum, "py", 0, 0, tiled=True)
    spectrum = spectrum.reshape(cols_dev, 2, span_kz, span_x, span_y)
    turn_y = complex_block(wave_cos, wave_sin, False).reshape(2, 2, rows_dev, span_ky, cols_dev, span_y)
    spectrum = jnp.einsum("dcilsy,sckxy->idlkx", turn_y, spectrum, precision=HIGH)
    spectrum = spectrum.reshape(rows_dev, 2, span_ky, span_kz * span_x)
    spectrum = lax.all_to_all(spectrum, "px", 0, 0, tiled=True)
    spectrum = spectrum.reshape(rows_dev, 2, span_ky, span_kz, span_x)
    turn_x = complex_block(wave_cos, wave_sin, False).reshape(2, 2, K, rows_dev, span_x)
    spectrum = jnp.einsum("dcqrx,rclkx->qdlk", turn_x, spectrum, precision=HIGH)
    wave_x = jnp.arange(K, dtype=jnp.int32)
    wave_y = index_x * span_ky + jnp.arange(span_ky, dtype=jnp.int32)
    wave_z = index_y * span_kz + jnp.arange(span_kz, dtype=jnp.int32)
    kernel = influence(wave_x[:, None, None], wave_y[None, :, None], wave_z[None, None, :], K) * (
        1.0 / float(K**3)
    )
    spectrum = spectrum * kernel[:, None]
    back_x = complex_block(wave_cos, wave_sin, True).reshape(2, 2, rows_dev, span_x, K)
    spectrum = jnp.einsum("dcrxq,qclk->rdlkx", back_x, spectrum, precision=HIGH)
    spectrum = spectrum.reshape(rows_dev, 2, span_ky, span_kz * span_x)
    spectrum = lax.all_to_all(spectrum, "px", 0, 0, tiled=True)
    spectrum = spectrum.reshape(rows_dev, 2, span_ky, span_kz, span_x)
    back_y = complex_block(wave_cos, wave_sin, True).reshape(2, 2, cols_dev, span_y, rows_dev, span_ky)
    spectrum = jnp.einsum("dcsyil,iclkx->sdkxy", back_y, spectrum, precision=HIGH)
    spectrum = spectrum.reshape(cols_dev, 2, span_kz, span_x * span_y)
    spectrum = lax.all_to_all(spectrum, "py", 0, 0, tiled=True)
    back_z = jnp.stack([wave_cos, -wave_sin], axis=1).reshape(K, 2, cols_dev, span_kz)
    potential = jnp.einsum("zcjk,jckm->mz", back_z, spectrum, precision=HIGH)
    potential = potential.reshape(span_x, span_y, K)
    lower_rows = from_behind(potential[:5], "px", -1)
    potential = jnp.concatenate([potential, lower_rows], axis=0)
    lower_cols = from_behind(potential[:, :5], "py", -1)
    gap = jnp.zeros((span_x + 5, pad_y - span_y - 5, K), jnp.float32)
    potential = jnp.concatenate([potential, lower_cols, gap], axis=1).reshape(-1, K)

    late_base, late_slopes = lax.optimization_barrier((base_z, slopes_z))
    both_z = jnp.concatenate([table_z, place_depth(late_base, late_slopes, K)], axis=0)
    sampled = lax.dot_general(
        potential, both_z, (((1,), (1,)), ((), ())), precision=HIGH
    ).reshape(span_x + 5, pad_y, 2, atoms)
    plain = sampled[:, :, 0]
    sloped = sampled[:, :, 1]
    force_x = jnp.sum(slope_x[:, None, :] * table_y[None, :, :] * plain, axis=(0, 1))
    force_y = jnp.sum(table_x[:, None, :] * slope_y[None, :, :] * plain, axis=(0, 1))
    force_z = jnp.sum(table_x[:, None, :] * table_y[None, :, :] * sloped, axis=(0, 1))
    pulled = (-amounts[None, :] * jnp.stack([force_x, force_y, force_z])).reshape(3, slots, width)
    pulled = pulled.transpose(1, 0, 2).reshape(cols_dev, capacity, 3, width)
    returned = lax.all_to_all(pulled, "py", split_axis=0, concat_axis=0, tiled=True).reshape(
        slots, 3, width
    )
    return jnp.take(returned, slot_of, axis=0) * alive[:, None, None]


def solution(mesh):
    placed = (
        P(("px", "py"), None, None),
        P(("px", "py"), None),
        P(("px", "py"), None),
        P(("px", "py"), None),
        P(("px", "py")),
    )
    return jax.shard_map(
        per_device,
        mesh=mesh,
        in_specs=placed,
        out_specs=P(("px", "py"), None, None),
        check_vma=False,
    )
```
